32 devices in a mesh: grp: 1, dap: 32 (over z, y, x, core).
Axes of the slice: x: 2, y: 2, z: 4, core: 2. Of those that a mesh axis runs over, the one named last changes fastest.
Arguments:
- alignment: bfloat16 [64, 128, 256], P(('grp', 'dap')), may hold values from -6 to 6
- pairwise: bfloat16 [128, 128, 128], P(('grp', 'dap')), may hold values from -6 to 6
- sequence_mask: int32 [64], P('grp'), may hold values from 0 to 1, as said below
- residue_mask: int32 [128], P('grp'), may hold values from 0 to 1, as said below
- row_project: bfloat16 [4, 256, 256], replicated, may hold values from -0.375 to 0.375
- row_bias_map: bfloat16 [128, 8], replicated, as said below
- row_output: bfloat16 [256, 256], replicated, may hold values from -0.375 to 0.375
- column_project: bfloat16 [4, 256, 256], replicated, as said below
- column_output: bfloat16 [256, 256], replicated, may hold values from -0.375 to 0.375
- start_project: bfloat16 [4, 128, 128], replicated, may hold values from -0.5 to 0.5
- start_bias_map: bfloat16 [128, 4], replicated, as said below
- start_output: bfloat16 [128, 128], replicated, may hold values from -0.5 to 0.5
- end_project: bfloat16 [4, 128, 128], replicated, may hold values from -0.5 to 0.5
- end_bias_map: bfloat16 [128, 4], replicated, as said below
- end_output: bfloat16 [128, 128], replicated, may hold values from -0.5 to 0.5
- outer_left: bfloat16 [256, 32], replicated, may hold values from -0.375 to 0.375
- outer_right: bfloat16 [256, 32], replicated, may hold values from -0.375 to 0.375
- outer_output: bfloat16 [1024, 128], replicated, may hold values from -1 to 1
Outputs:
- alignment_out: bfloat16 [64, 128, 256], P('grp', 'dap')
- pairwise_out: bfloat16 [128, 128, 128], P('grp', 'dap')
The draws below stay inside these ranges and needn't reach their ends.
Inputs may be any that keep to these rules, and one draw needn't show every extreme that they name: `sequence_mask`: 0 or 1; entry 0, the query sequence, is always 1. `residue_mask`: 1 on a prefix of the residues of 64 positions or more, 0 after it. `row_bias_map`: a weight matrix. `start_bias_map`: a weight matrix. `end_bias_map`: a weight matrix. `column_project`: weight matrices.
All inputs are finite; a program needn't handle non-finite values.
Results may differ from the reference program's by a relative error of at most 0.02.
The reference program's roundings to bfloat16 on the way count: a program that leaves them out, or rounds other values in their place, can miss the bound.
Values may be sent and summed in bfloat16 or wider, within the bound.
No kernel may reach another device: no remote copies, remote signals or barrier semaphores. Data moves between devices by JAX's collectives and lax.ppermute only.
A program may use at most 128 MiB of HBM per device.

```python
import jax
import jax.numpy as jnp
from jax import lax

C_M = 256
C_Z = 128
H_M = 8
H_Z = 4
DH = 32
C_O = 32
S = 64
L = 128


def scaled_weight(key, extent, fan_in):
    values = jax.random.normal(key, extent, jnp.float32) * fan_in ** (-0.5)
    return values


def draw_row_bias_map(key, part):
    return scaled_weight(jax.random.fold_in(key, 11), (C_Z, H_M), C_Z).astype(jnp.bfloat16)


def draw_start_bias_map(key, part):
    return scaled_weight(jax.random.fold_in(key, 23), (C_Z, H_Z), C_Z).astype(jnp.bfloat16)


def draw_end_bias_map(key, part):
    return scaled_weight(jax.random.fold_in(key, 37), (C_Z, H_Z), C_Z).astype(jnp.bfloat16)


def draw_column_project(key, part):
    values = jax.random.normal(jax.random.fold_in(key, 41), (4, C_M, H_M * DH), jnp.float32) * C_M ** (-0.5)
    return values.astype(jnp.bfloat16)


def draw_sequence_mask(key, part):
    picks = jax.random.randint(jax.random.fold_in(key, 53), (S,), 0, 4)
    kept = jnp.where(picks > 0, 1, 0)
    return jnp.where(jnp.arange(S) == 0, 1, kept).astype(jnp.int32)


def draw_residue_mask(key, part):
    length = L // 2 + jax.random.randint(jax.random.fold_in(key, 67), (), 0, L // 2 + 1)
    return jnp.where(jnp.arange(L) < length, 1, 0).astype(jnp.int32)


def block_scale(rng, shape, cuts, smallest, top_value):
    def one(position, parts):
        steps = jax.random.uniform(jax.random.fold_in(jax.random.fold_in(rng, 6), position), (parts,), jnp.float32, smallest / len(cuts), top_value / len(cuts))
        return jnp.repeat(jnp.exp(steps), shape[position] // parts).reshape((-1,) + (1,) * (len(shape) - position - 1))

    factor_of = one(*cuts[0])
    for cut in cuts[1:]:
        factor_of = factor_of * one(*cut)
    return factor_of


def scatter_about(own_key, shape, deviation, most, cuts=(), held_as=jnp.bfloat16):
    array = jax.random.normal(own_key, shape, jnp.float32) * deviation
    if len(cuts) > 0:
        array = block_scale(own_key, shape, cuts, -0.22, 0.18) * array
    return jnp.clip(array, min=-most, max=most).astype(held_as)


def setup_inputs(seed: int = 0, part: int = 0) -> dict:
    seeds = jax.random.split(jax.random.key(seed), 19)
    part_splits = jax.random.split(jax.random.fold_in(seeds[18], part), 19)
    return {
        "alignment": scatter_about(part_splits[0], (S, L, C_M), 1.0, 6.0, ((0, 32),)),
        "pairwise": scatter_about(part_splits[1], (L, L, C_Z), 1.0, 6.0, ((0, 32),)),
        "sequence_mask": draw_sequence_mask(jax.random.fold_in(jax.random.fold_in(seeds[18], part), 71), part),
        "residue_mask": draw_residue_mask(jax.random.fold_in(jax.random.fold_in(seeds[18], part), 71), part),
        "row_project": scatter_about(seeds[4], (4, C_M, H_M * DH), C_M ** -0.5, 0.375),
        "row_bias_map": draw_row_bias_map(jax.random.fold_in(seeds[18], 71), part),
        "row_output": scatter_about(seeds[6], (H_M * DH, C_M), (H_M * DH) ** -0.5, 0.375),
        "column_project": draw_column_project(jax.random.fold_in(seeds[18], 71), part),
        "column_output": scatter_about(seeds[8], (H_M * DH, C_M), (H_M * DH) ** -0.5, 0.375),
        "start_project": scatter_about(seeds[9], (4, C_Z, H_Z * DH), C_Z ** -0.5, 0.5),
        "start_bias_map": draw_start_bias_map(jax.random.fold_in(seeds[18], 71), part),
        "start_output": scatter_about(seeds[11], (H_Z * DH, C_Z), (H_Z * DH) ** -0.5, 0.5),
        "end_project": scatter_about(seeds[12], (4, C_Z, H_Z * DH), C_Z ** -0.5, 0.5),
        "end_bias_map": draw_end_bias_map(jax.random.fold_in(seeds[18], 71), part),
        "end_output": scatter_about(seeds[14], (H_Z * DH, C_Z), (H_Z * DH) ** -0.5, 0.5),
        "outer_left": scatter_about(seeds[15], (C_M, C_O), C_M ** -0.5, 0.375),
        "outer_right": scatter_about(seeds[16], (C_M, C_O), C_M ** -0.5, 0.375),
        "outer_output": scatter_about(seeds[17], (C_O * C_O, C_Z), C_O ** -0.5, 1.0),
    }


norm_epsilon = 1e-05
mask_scale = 1000000000.0

def layer_norm(values):
    widened = values.astype(jnp.float32)
    center = widened - lax.optimization_barrier(jnp.mean(widened, axis=-1, keepdims=True))
    spread = lax.optimization_barrier(jnp.mean(center * center, axis=-1, keepdims=True))
    return (center * lax.rsqrt(spread + norm_epsilon)).astype(jnp.bfloat16)

def key_offsets(mask_values):
    return (mask_values.astype(jnp.float32) - 1.0) * mask_scale

def project(inputs, weight_table):
    return jnp.einsum('bqc,cf->bqf', inputs.astype(jnp.float32), weight_table.astype(jnp.float32))

def attend(inputs, weights, bias_table, key_bias, output_map, head_count):
    batch_size, query_count, width = inputs.shape
    query_all = project(inputs, weights[0]).astype(jnp.bfloat16)
    key_all = project(inputs, weights[1]).astype(jnp.bfloat16)
    value_all = project(inputs, weights[2]).astype(jnp.bfloat16)
    gating = jax.nn.sigmoid(project(inputs, weights[3]))
    head_size = query_all.shape[-1] // head_count
    query_heads = query_all.reshape(batch_size, query_count, head_count, head_size).astype(jnp.float32)
    key_heads = key_all.reshape(batch_size, query_count, head_count, head_size).astype(jnp.float32)
    value_heads = value_all.reshape(batch_size, query_count, head_count, head_size).astype(jnp.float32)
    scores = jnp.einsum('bqhd,bkhd->bhqk', query_heads, key_heads) * head_size ** (-0.5)
    if bias_table is not None:
        scores = scores + bias_table.astype(jnp.float32)[None]
    scores = scores + key_bias
    softened = jax.nn.softmax(scores, axis=-1).astype(jnp.bfloat16)
    mixed = jnp.einsum('bhqk,bkhd->bqhd', softened.astype(jnp.float32), value_heads)
    mixed = mixed.reshape(batch_size, query_count, head_count * head_size)
    gated = (mixed * gating).astype(jnp.bfloat16)
    return jnp.einsum('bqf,fc->bqc', gated.astype(jnp.float32), output_map.astype(jnp.float32))

def reference(alignment, pairwise, sequence_mask, residue_mask, row_project, row_bias_map, row_output, column_project, column_output, start_project, start_bias_map, start_output, end_project, end_bias_map, end_output, outer_left, outer_right, outer_output):
    residue_keys = key_offsets(residue_mask)
    sequence_keys = key_offsets(sequence_mask)
    pair_norm = layer_norm(pairwise)
    row_bias = jnp.einsum('ijc,ch->hij', pair_norm.astype(jnp.float32), row_bias_map.astype(jnp.float32)).astype(jnp.bfloat16)
    start_bias = jnp.einsum('ijc,ch->hij', pair_norm.astype(jnp.float32), start_bias_map.astype(jnp.float32)).astype(jnp.bfloat16)

    def row_step(row_slice):
        return attend(row_slice[None], row_project, row_bias, residue_keys, row_output, H_M)[0]
    alignment_one = (alignment.astype(jnp.float32) + lax.map(row_step, layer_norm(alignment))).astype(jnp.bfloat16)
    column_norm = jnp.swapaxes(layer_norm(alignment_one), 0, 1)

    def column_step(row_slice):
        return attend(row_slice[None], column_project, None, sequence_keys, column_output, H_M)[0]
    column_update = jnp.swapaxes(lax.map(column_step, column_norm), 0, 1)
    alignment_out = (alignment_one.astype(jnp.float32) + column_update).astype(jnp.bfloat16)

    def start_step(row_slice):
        return attend(row_slice[None], start_project, start_bias, residue_keys, start_output, H_Z)[0]
    pair_one = (pairwise.astype(jnp.float32) + lax.map(start_step, pair_norm)).astype(jnp.bfloat16)
    pair_norm_one = layer_norm(pair_one)
    end_bias = jnp.einsum('kic,ch->hik', pair_norm_one.astype(jnp.float32), end_bias_map.astype(jnp.float32)).astype(jnp.bfloat16)

    def end_step(row_slice):
        return attend(row_slice[None], end_project, end_bias, residue_keys, end_output, H_Z)[0]
    end_update = jnp.swapaxes(lax.map(end_step, jnp.swapaxes(pair_norm_one, 0, 1)), 0, 1)
    last_norm = layer_norm(alignment_out).astype(jnp.float32)
    weighting = sequence_mask.astype(jnp.float32)[:, None, None]
    left = (jnp.einsum('sic,co->sio', last_norm, outer_left.astype(jnp.float32)) * weighting).astype(jnp.bfloat16)
    right = (jnp.einsum('sic,co->sio', last_norm, outer_right.astype(jnp.float32)) * weighting).astype(jnp.bfloat16)
    row_count = jnp.sum(sequence_mask.astype(jnp.float32))
    right_wide = right.astype(jnp.float32)

    def outer_step(column_left):
        outer_sum = jnp.einsum('sc,sje->jce', column_left.astype(jnp.float32), right_wide) / row_count
        flattened = outer_sum.astype(jnp.bfloat16).reshape(outer_sum.shape[0], -1)
        return jnp.dot(flattened, outer_output, preferred_element_type=jnp.float32)
    outer_update = lax.map(outer_step, jnp.swapaxes(left, 0, 1))
    pairwise_out = (pair_one.astype(jnp.float32) + end_update + outer_update).astype(jnp.bfloat16)
    return (alignment_out, pairwise_out)
```

```python
import functools

import jax
import jax.numpy as jnp
from jax import lax
from jax.sharding import PartitionSpec as P

H_M = 8
H_Z = 4


norm_epsilon = 1e-05
mask_scale = 1000000000.0


def layer_norm(values):
    widened = values.astype(jnp.float32)
    center = widened - jnp.mean(widened, axis=-1, keepdims=True)
    spread = jnp.mean(center * center, axis=-1, keepdims=True)
    return (center * lax.rsqrt(spread + norm_epsilon)).astype(jnp.bfloat16)


def key_offsets(mask_values):
    return (mask_values.astype(jnp.float32) - 1.0) * mask_scale


def project(inputs, weight_table):
    return jnp.einsum("bqc,cf->bqf", inputs, weight_table, preferred_element_type=jnp.float32)


def attend(inputs, weights, bias_table, key_bias, output_map, head_count):
    batch_size, query_count, width = inputs.shape
    query_all = project(inputs, weights[0]).astype(jnp.bfloat16)
    key_all = project(inputs, weights[1]).astype(jnp.bfloat16)
    value_all = project(inputs, weights[2]).astype(jnp.bfloat16)
    gating = jax.nn.sigmoid(project(inputs, weights[3]))
    head_size = query_all.shape[-1] // head_count
    query_heads = query_all.reshape(batch_size, query_count, head_count, head_size)
    key_heads = key_all.reshape(batch_size, query_count, head_count, head_size)
    value_heads = value_all.reshape(batch_size, query_count, head_count, head_size)
    scores = jnp.einsum(
        "bqhd,bkhd->bhqk", query_heads, key_heads, preferred_element_type=jnp.float32
    ) * head_size ** (-0.5)
    if bias_table is not None:
        scores = scores + bias_table.astype(jnp.float32)[None]
    scores = scores + key_bias
    softened = jax.nn.softmax(scores, axis=-1).astype(jnp.bfloat16)
    mixed = jnp.einsum("bhqk,bkhd->bqhd", softened, value_heads, preferred_element_type=jnp.float32)
    mixed = mixed.reshape(batch_size, query_count, head_count * head_size)
    gated = (mixed * gating).astype(jnp.bfloat16)
    return jnp.einsum("bqf,fc->bqc", gated, output_map, preferred_element_type=jnp.float32)


def gather_blocks(block, axis, count):
    spread = jnp.broadcast_to(block[None], (count,) + block.shape)
    received = lax.all_to_all(spread, "dap", 0, 0, tiled=True)
    received = jnp.moveaxis(received, 0, axis)
    shape = block.shape[:axis] + (count * block.shape[axis],) + block.shape[axis + 1 :]
    return received.reshape(shape)


def per_device(
    alignment,
    pairwise,
    sequence_mask,
    residue_mask,
    row_project,
    row_bias_map,
    row_output,
    column_project,
    column_output,
    start_project,
    start_bias_map,
    start_output,
    end_project,
    end_bias_map,
    end_output,
    outer_left,
    outer_right,
    outer_output,
    count=1,
):
    residue_keys = key_offsets(residue_mask)
    sequence_keys = key_offsets(sequence_mask)
    pair_norm = layer_norm(pairwise)
    both_maps = jnp.concatenate([row_bias_map, start_bias_map], axis=1)
    both_local = jnp.einsum(
        "ijc,ch->hij", pair_norm, both_maps, preferred_element_type=jnp.float32
    ).astype(jnp.bfloat16)
    both_bias = gather_blocks(both_local, 1, count)
    row_bias = both_bias[:H_M]
    start_bias = both_bias[H_M:]
    row_update = attend(layer_norm(alignment), row_project, row_bias, residue_keys, row_output, H_M)
    alignment_one = (alignment.astype(jnp.float32) + row_update).astype(jnp.bfloat16)
    alignment_cols = lax.all_to_all(alignment_one, "dap", split_axis=1, concat_axis=0, tiled=True)
    start_update = attend(pair_norm, start_project, start_bias, residue_keys, start_output, H_Z)
    pair_one = (pairwise.astype(jnp.float32) + start_update).astype(jnp.bfloat16)
    pair_cols = lax.all_to_all(pair_one, "dap", split_axis=1, concat_axis=0, tiled=True)
    rows_norm_one = layer_norm(pair_one)
    end_local = jnp.einsum(
        "kic,ch->hki", rows_norm_one, end_bias_map, preferred_element_type=jnp.float32
    ).astype(jnp.bfloat16)
    end_bias = jnp.swapaxes(gather_blocks(end_local, 1, count), 1, 2)
    column_norm = jnp.swapaxes(layer_norm(alignment_cols), 0, 1)
    column_update = attend(column_norm, column_project, None, sequence_keys, column_output, H_M)
    alignment_out = (alignment_cols.astype(jnp.float32) + jnp.swapaxes(column_update, 0, 1)).astype(
        jnp.bfloat16
    )
    end_norm = jnp.swapaxes(layer_norm(pair_cols), 0, 1)
    end_update = jnp.swapaxes(
        attend(end_norm, end_project, end_bias, residue_keys, end_output, H_Z), 0, 1
    )
    last_norm = layer_norm(alignment_out)
    weighting = sequence_mask.astype(jnp.float32)[:, None, None]
    left = (
        jnp.einsum("sic,co->sio", last_norm, outer_left, preferred_element_type=jnp.float32)
        * weighting
    ).astype(jnp.bfloat16)
    right = (
        jnp.einsum("sic,co->sio", last_norm, outer_right, preferred_element_type=jnp.float32)
        * weighting
    ).astype(jnp.bfloat16)
    row_count = jnp.sum(sequence_mask.astype(jnp.float32))
    outer_sum = (
        jnp.einsum(
            "sic,sje->ijce",
            gather_blocks(left, 1, count),
            right,
            preferred_element_type=jnp.float32,
        )
        / row_count
    )
    flattened = outer_sum.astype(jnp.bfloat16).reshape(outer_sum.shape[0], outer_sum.shape[1], -1)
    outer_update = jnp.einsum(
        "ijf,fc->ijc", flattened, outer_output, preferred_element_type=jnp.float32
    )
    pairwise_out = (pair_cols.astype(jnp.float32) + end_update + outer_update).astype(jnp.bfloat16)
    return (alignment_out, pairwise_out)


def solution(mesh):
    return jax.shard_map(
        functools.partial(per_device, count=mesh.shape["dap"]),
        mesh=mesh,
        in_specs=(
            P(("grp", "dap"), None, None),
            P(("grp", "dap"), None, None),
            P("grp"),
            P("grp"),
            P(),
            P(),
            P(),
            P(),
            P(),
            P(),
            P(),
            P(),
            P(),
            P(),
            P(),
            P(),
            P(),
            P(),
        ),
        out_specs=(P("grp", "dap", None), P("grp", "dap", None)),
        check_vma=False,
    )
```

```python
import functools

import jax
import jax.numpy as jnp
from jax import lax
from jax.sharding import PartitionSpec as P

H_M = 8
H_Z = 4


norm_epsilon = 1e-05
mask_scale = 1000000000.0


def layer_norm(values):
    widened = values.astype(jnp.float32)
    center = widened - jnp.mean(widened, axis=-1, keepdims=True)
    spread = jnp.mean(center * center, axis=-1, keepdims=True)
    return (center * lax.rsqrt(spread + norm_epsilon)).astype(jnp.bfloat16)


def key_offsets(mask_values):
    return (mask_values.astype(jnp.float32) - 1.0) * mask_scale


def project(inputs, weight_table):
    return jnp.einsum("bqc,cf->bqf", inputs, weight_table, preferred_element_type=jnp.float32)


def attend(inputs, weights, bias_table, key_bias, output_map, head_count):
    batch_size, query_count, width = inputs.shape
    query_all = project(inputs, weights[0]).astype(jnp.bfloat16)
    key_all = project(inputs, weights[1]).astype(jnp.bfloat16)
    value_all = project(inputs, weights[2]).astype(jnp.bfloat16)
    gating = jax.nn.sigmoid(project(inputs, weights[3]))
    head_size = query_all.shape[-1] // head_count
    query_heads = query_all.reshape(batch_size, query_count, head_count, head_size)
    key_heads = key_all.reshape(batch_size, query_count, head_count, head_size)
    value_heads = value_all.reshape(batch_size, query_count, head_count, head_size)
    scores = jnp.einsum(
        "bqhd,bkhd->bhqk", query_heads, key_heads, preferred_element_type=jnp.float32
    ) * head_size ** (-0.5)
    if bias_table is not None:
        scores = scores + bias_table.astype(jnp.float32)[None]
    scores = scores + key_bias
    softened = jax.nn.softmax(scores, axis=-1).astype(jnp.bfloat16)
    mixed = jnp.einsum("bhqk,bkhd->bqhd", softened, value_heads, preferred_element_type=jnp.float32)
    mixed = mixed.reshape(batch_size, query_count, head_count * head_size)
    gated = (mixed * gating).astype(jnp.bfloat16)
    return jnp.einsum("bqf,fc->bqc", gated, output_map, preferred_element_type=jnp.float32)


def gather_blocks(block, axis, count):
    spread = jnp.broadcast_to(block[None], (count,) + block.shape)
    received = lax.all_to_all(spread, "dap", 0, 0, tiled=True)
    received = jnp.moveaxis(received, 0, axis)
    shape = block.shape[:axis] + (count * block.shape[axis],) + block.shape[axis + 1 :]
    return received.reshape(shape)


def split_for_all(values, count):
    lead, width = values.shape[0], values.shape[1]
    pieces = values.reshape((lead, count, width // count) + values.shape[2:])
    return jnp.moveaxis(pieces, 1, 0).reshape(count, -1)


def exchange(alignment_one, pair_one, end_local, count):
    parts = [
        split_for_all(alignment_one, count),
        split_for_all(pair_one, count),
        jnp.broadcast_to(end_local.reshape(1, -1), (count, end_local.size)),
    ]
    sizes = [part.shape[1] for part in parts]
    received = lax.all_to_all(jnp.concatenate(parts, axis=1), "dap", 0, 0, tiled=True)
    first, second = sizes[0], sizes[0] + sizes[1]
    block = alignment_one.shape[1] // count
    alignment_cols = received[:, :first].reshape(
        (count * alignment_one.shape[0], block) + alignment_one.shape[2:]
    )
    pair_cols = received[:, first:second].reshape(
        (count * pair_one.shape[0], block) + pair_one.shape[2:]
    )
    end_all = jnp.moveaxis(received[:, second:].reshape((count,) + end_local.shape), 0, 1)
    end_all = end_all.reshape(
        (end_local.shape[0], count * end_local.shape[1]) + end_local.shape[2:]
    )
    return alignment_cols, pair_cols, end_all


def per_device(
    alignment,
    pairwise,
    sequence_mask,
    residue_mask,
    row_project,
    row_bias_map,
    row_output,
    column_project,
    column_output,
    start_project,
    start_bias_map,
    start_output,
    end_project,
    end_bias_map,
    end_output,
    outer_left,
    outer_right,
    outer_output,
    count=1,
):
    residue_keys = key_offsets(residue_mask)
    sequence_keys = key_offsets(sequence_mask)
    pair_norm = layer_norm(pairwise)
    both_maps = jnp.concatenate([row_bias_map, start_bias_map], axis=1)
    both_local = jnp.einsum(
        "ijc,ch->hij", pair_norm, both_maps, preferred_element_type=jnp.float32
    ).astype(jnp.bfloat16)
    both_bias = gather_blocks(both_local, 1, count)
    row_bias = both_bias[:H_M]
    start_bias = both_bias[H_M:]
    row_update = attend(layer_norm(alignment), row_project, row_bias, residue_keys, row_output, H_M)
    alignment_one = (alignment.astype(jnp.float32) + row_update).astype(jnp.bfloat16)
    start_update = attend(pair_norm, start_project, start_bias, residue_keys, start_output, H_Z)
    pair_one = (pairwise.astype(jnp.float32) + start_update).astype(jnp.bfloat16)
    rows_norm_one = layer_norm(pair_one)
    end_local = jnp.einsum(
        "kic,ch->hki", rows_norm_one, end_bias_map, preferred_element_type=jnp.float32
    ).astype(jnp.bfloat16)
    alignment_cols, pair_cols, end_all = exchange(alignment_one, pair_one, end_local, count)
    end_bias = jnp.swapaxes(end_all, 1, 2)
    column_norm = jnp.swapaxes(layer_norm(alignment_cols), 0, 1)
    column_update = attend(column_norm, column_project, None, sequence_keys, column_output, H_M)
    alignment_out = (alignment_cols.astype(jnp.float32) + jnp.swapaxes(column_update, 0, 1)).astype(
        jnp.bfloat16
    )
    end_norm = jnp.swapaxes(layer_norm(pair_cols), 0, 1)
    end_update = jnp.swapaxes(
        attend(end_norm, end_project, end_bias, residue_keys, end_output, H_Z), 0, 1
    )
    last_norm = layer_norm(alignment_out)
    weighting = sequence_mask.astype(jnp.float32)[:, None, None]
    left = (
        jnp.einsum("sic,co->sio", last_norm, outer_left, preferred_element_type=jnp.float32)
        * weighting
    ).astype(jnp.bfloat16)
    right = (
        jnp.einsum("sic,co->sio", last_norm, outer_right, preferred_element_type=jnp.float32)
        * weighting
    ).astype(jnp.bfloat16)
    row_count = jnp.sum(sequence_mask.astype(jnp.float32))
    outer_sum = (
        jnp.einsum(
            "sic,sje->ijce",
            gather_blocks(left, 1, count),
            right,
            preferred_element_type=jnp.float32,
        )
        / row_count
    )
    flattened = outer_sum.astype(jnp.bfloat16).reshape(outer_sum.shape[0], outer_sum.shape[1], -1)
    outer_update = jnp.einsum(
        "ijf,fc->ijc", flattened, outer_output, preferred_element_type=jnp.float32
    )
    pairwise_out = (pair_cols.astype(jnp.float32) + end_update + outer_update).astype(jnp.bfloat16)
    return (alignment_out, pairwise_out)


def solution(mesh):
    return jax.shard_map(
        functools.partial(per_device, count=mesh.shape["dap"]),
        mesh=mesh,
        in_specs=(
            P(("grp", "dap"), None, None),
            P(("grp", "dap"), None, None),
            P("grp"),
            P("grp"),
            P(),
            P(),
            P(),
            P(),
            P(),
            P(),
            P(),
            P(),
            P(),
            P(),
            P(),
            P(),
            P(),
            P(),
        ),
        out_specs=(P("grp", "dap", None), P("grp", "dap", None)),
        check_vma=False,
    )
```

```python
import functools

import jax
import jax.numpy as jnp
from jax import lax
from jax.sharding import PartitionSpec as P

H_M = 8
H_Z = 4


norm_epsilon = 1e-05
mask_scale = 1000000000.0


def layer_norm(values):
    widened = values.astype(jnp.float32)
    center = widened - jnp.mean(widened, axis=-1, keepdims=True)
    spread = jnp.mean(center * center, axis=-1, keepdims=True)
    return (center * lax.rsqrt(spread + norm_epsilon)).astype(jnp.bfloat16)


def key_offsets(mask_values):
    return (mask_values.astype(jnp.float32) - 1.0) * mask_scale


def project(inputs, weight_table):
    return jnp.einsum("bqc,cf->bqf", inputs, weight_table, preferred_element_type=jnp.float32)


def attend(inputs, weights, bias_table, key_bias, output_map, head_count):
    batch_size, query_count, width = inputs.shape
    query_all = project(inputs, weights[0]).astype(jnp.bfloat16)
    key_all = project(inputs, weights[1]).astype(jnp.bfloat16)
    value_all = project(inputs, weights[2]).astype(jnp.bfloat16)
    gating = jax.nn.sigmoid(project(inputs, weights[3]))
    head_size = query_all.shape[-1] // head_count
    query_heads = query_all.reshape(batch_size, query_count, head_count, head_size)
    key_heads = key_all.reshape(batch_size, query_count, head_count, head_size)
    value_heads = value_all.reshape(batch_size, query_count, head_count, head_size)
    scores = jnp.einsum(
        "bqhd,bkhd->bhqk", query_heads, key_heads, preferred_element_type=jnp.float32
    ) * head_size ** (-0.5)
    if bias_table is not None:
        scores = scores + bias_table.astype(jnp.float32)[None]
    scores = scores + key_bias
    softened = jax.nn.softmax(scores, axis=-1).astype(jnp.bfloat16)
    mixed = jnp.einsum("bhqk,bkhd->bqhd", softened, value_heads, preferred_element_type=jnp.float32)
    mixed = mixed.reshape(batch_size, query_count, head_count * head_size)
    gated = (mixed * gating).astype(jnp.bfloat16)
    return jnp.einsum("bqf,fc->bqc", gated, output_map, preferred_element_type=jnp.float32)


def gather_blocks(block, axis, count):
    spread = jnp.broadcast_to(block[None], (count,) + block.shape)
    received = lax.all_to_all(spread, "dap", 0, 0, tiled=True)
    received = jnp.moveaxis(received, 0, axis)
    shape = block.shape[:axis] + (count * block.shape[axis],) + block.shape[axis + 1 :]
    return received.reshape(shape)


def split_for_all(values, count):
    lead, width = values.shape[0], values.shape[1]
    pieces = values.reshape((lead, count, width // count) + values.shape[2:])
    return jnp.moveaxis(pieces, 1, 0).reshape(count, -1)


def exchange(blocks, broadcast, count):
    parts = [split_for_all(values, count) for values in blocks]
    if broadcast is not None:
        parts.append(jnp.broadcast_to(broadcast.reshape(1, -1), (count, broadcast.size)))
    received = lax.all_to_all(jnp.concatenate(parts, axis=1), "dap", 0, 0, tiled=True)
    results, offset = [], 0
    for values, part in zip(blocks, parts):
        block = values.shape[1] // count
        piece = received[:, offset : offset + part.shape[1]]
        results.append(piece.reshape((count * values.shape[0], block) + values.shape[2:]))
        offset += part.shape[1]
    if broadcast is not None:
        gathered = jnp.moveaxis(received[:, offset:].reshape((count,) + broadcast.shape), 0, 1)
        results.append(
            gathered.reshape((broadcast.shape[0], count * broadcast.shape[1]) + broadcast.shape[2:])
        )
    return results


def per_device(
    alignment,
    pairwise,
    sequence_mask,
    residue_mask,
    row_project,
    row_bias_map,
    row_output,
    column_project,
    column_output,
    start_project,
    start_bias_map,
    start_output,
    end_project,
    end_bias_map,
    end_output,
    outer_left,
    outer_right,
    outer_output,
    count=1,
):
    residue_keys = key_offsets(residue_mask)
    sequence_keys = key_offsets(sequence_mask)
    pair_norm = layer_norm(pairwise)
    both_maps = jnp.concatenate([row_bias_map, start_bias_map], axis=1)
    both_local = jnp.einsum(
        "ijc,ch->hij", pair_norm, both_maps, preferred_element_type=jnp.float32
    ).astype(jnp.bfloat16)
    both_bias = gather_blocks(both_local, 1, count)
    row_bias = both_bias[:H_M]
    start_bias = both_bias[H_M:]
    row_update = attend(layer_norm(alignment), row_project, row_bias, residue_keys, row_output, H_M)
    alignment_one = (alignment.astype(jnp.float32) + row_update).astype(jnp.bfloat16)
    (alignment_cols,) = exchange([alignment_one], None, count)
    start_update = attend(pair_norm, start_project, start_bias, residue_keys, start_output, H_Z)
    pair_one = (pairwise.astype(jnp.float32) + start_update).astype(jnp.bfloat16)
    rows_norm_one = layer_norm(pair_one)
    end_local = jnp.einsum(
        "kic,ch->hki", rows_norm_one, end_bias_map, preferred_element_type=jnp.float32
    ).astype(jnp.bfloat16)
    pair_cols, end_all = exchange([pair_one], end_local, count)
    end_bias = jnp.swapaxes(end_all, 1, 2)
    column_norm = jnp.swapaxes(layer_norm(alignment_cols), 0, 1)
    column_update = attend(column_norm, column_project, None, sequence_keys, column_output, H_M)
    alignment_out = (alignment_cols.astype(jnp.float32) + jnp.swapaxes(column_update, 0, 1)).astype(
        jnp.bfloat16
    )
    end_norm = jnp.swapaxes(layer_norm(pair_cols), 0, 1)
    end_update = jnp.swapaxes(
        attend(end_norm, end_project, end_bias, residue_keys, end_output, H_Z), 0, 1
    )
    last_norm = layer_norm(alignment_out)
    weighting = sequence_mask.astype(jnp.float32)[:, None, None]
    left = (
        jnp.einsum("sic,co->sio", last_norm, outer_left, preferred_element_type=jnp.float32)
        * weighting
    ).astype(jnp.bfloat16)
    right = (
        jnp.einsum("sic,co->sio", last_norm, outer_right, preferred_element_type=jnp.float32)
        * weighting
    ).astype(jnp.bfloat16)
    row_count = jnp.sum(sequence_mask.astype(jnp.float32))
    outer_sum = (
        jnp.einsum(
            "sic,sje->ijce",
            gather_blocks(left, 1, count),
            right,
            preferred_element_type=jnp.float32,
        )
        / row_count
    )
    flattened = outer_sum.astype(jnp.bfloat16).reshape(outer_sum.shape[0], outer_sum.shape[1], -1)
    outer_update = jnp.einsum(
        "ijf,fc->ijc", flattened, outer_output, preferred_element_type=jnp.float32
    )
    pairwise_out = (pair_cols.astype(jnp.float32) + end_update + outer_update).astype(jnp.bfloat16)
    return (alignment_out, pairwise_out)


def solution(mesh):
    return jax.shard_map(
        functools.partial(per_device, count=mesh.shape["dap"]),
        mesh=mesh,
        in_specs=(
            P(("grp", "dap"), None, None),
            P(("grp", "dap"), None, None),
            P("grp"),
            P("grp"),
            P(),
            P(),
            P(),
            P(),
            P(),
            P(),
            P(),
            P(),
            P(),
            P(),
            P(),
            P(),
            P(),
            P(),
        ),
        out_specs=(P("grp", "dap", None), P("grp", "dap", None)),
        check_vma=False,
    )
```

```python
import functools

import jax
import jax.numpy as jnp
from jax import lax
from jax.sharding import PartitionSpec as P

H_M = 8
H_Z = 4


norm_epsilon = 1e-05
mask_scale = 1000000000.0


def layer_norm(values):
    widened = values.astype(jnp.float32)
    center = widened - jnp.mean(widened, axis=-1, keepdims=True)
    spread = jnp.mean(center * center, axis=-1, keepdims=True)
    return (center * lax.rsqrt(spread + norm_epsilon)).astype(jnp.bfloat16)


def key_offsets(mask_values):
    return (mask_values.astype(jnp.float32) - 1.0) * mask_scale


def project(inputs, weight_table):
    return jnp.einsum("bqc,cf->bqf", inputs, weight_table, preferred_element_type=jnp.float32)


def attend(inputs, weights, bias_table, key_bias, output_map, head_count):
    batch_size, query_count, width = inputs.shape
    query_all = project(inputs, weights[0]).astype(jnp.bfloat16)
    key_all = project(inputs, weights[1]).astype(jnp.bfloat16)
    value_all = project(inputs, weights[2]).astype(jnp.bfloat16)
    gating = jax.nn.sigmoid(project(inputs, weights[3]))
    head_size = query_all.shape[-1] // head_count
    query_heads = query_all.reshape(batch_size, query_count, head_count, head_size)
    key_heads = key_all.reshape(batch_size, query_count, head_count, head_size)
    value_heads = value_all.reshape(batch_size, query_count, head_count, head_size)
    scores = jnp.einsum(
        "bqhd,bkhd->bhqk", query_heads, key_heads, preferred_element_type=jnp.float32
    ) * head_size ** (-0.5)
    if bias_table is not None:
        scores = scores + bias_table.astype(jnp.float32)[None]
    scores = scores + key_bias
    softened = jax.nn.softmax(scores, axis=-1).astype(jnp.bfloat16)
    mixed = jnp.einsum("bhqk,bkhd->bqhd", softened, value_heads, preferred_element_type=jnp.float32)
    mixed = mixed.reshape(batch_size, query_count, head_count * head_size)
    gated = (mixed * gating).astype(jnp.bfloat16)
    return jnp.einsum("bqf,fc->bqc", gated, output_map, preferred_element_type=jnp.float32)


def gather_blocks(block, axis, count):
    spread = jnp.broadcast_to(block[None], (count,) + block.shape)
    received = lax.all_to_all(spread, "dap", 0, 0, tiled=True)
    received = jnp.moveaxis(received, 0, axis)
    shape = block.shape[:axis] + (count * block.shape[axis],) + block.shape[axis + 1 :]
    return received.reshape(shape)


def exchange_pair(pair_one, end_local, count):
    rows, width, channels = pair_one.shape
    block = width // count
    pair_part = jnp.moveaxis(pair_one.reshape(rows, count, block, channels), 1, 0)
    pair_part = pair_part.reshape(count, rows * block, channels)
    end_part = jnp.broadcast_to(
        end_local.reshape(1, -1, channels), (count, end_local.size // channels, channels)
    )
    received = lax.all_to_all(
        jnp.concatenate([pair_part, end_part], axis=1), "dap", 0, 0, tiled=True
    )
    pair_cols = received[:, : rows * block].reshape(count * rows, block, channels)
    end_all = received[:, rows * block :].reshape((count,) + end_local.shape)
    end_all = jnp.moveaxis(end_all, 0, 1).reshape(
        (end_local.shape[0], count * end_local.shape[1]) + end_local.shape[2:]
    )
    return pair_cols, end_all


def per_device(
    alignment,
    pairwise,
    sequence_mask,
    residue_mask,
    row_project,
    row_bias_map,
    row_output,
    column_project,
    column_output,
    start_project,
    start_bias_map,
    start_output,
    end_project,
    end_bias_map,
    end_output,
    outer_left,
    outer_right,
    outer_output,
    count=1,
):
    residue_keys = key_offsets(residue_mask)
    sequence_keys = key_offsets(sequence_mask)
    pair_norm = layer_norm(pairwise)
    both_maps = jnp.concatenate([row_bias_map, start_bias_map], axis=1)
    both_local = jnp.einsum(
        "ijc,ch->hij", pair_norm, both_maps, preferred_element_type=jnp.float32
    ).astype(jnp.bfloat16)
    both_bias = gather_blocks(both_local, 1, count)
    row_bias = both_bias[:H_M]
    start_bias = both_bias[H_M:]
    row_update = attend(layer_norm(alignment), row_project, row_bias, residue_keys, row_output, H_M)
    alignment_one = (alignment.astype(jnp.float32) + row_update).astype(jnp.bfloat16)
    alignment_cols = lax.all_to_all(alignment_one, "dap", 1, 0, tiled=True)
    start_update = attend(pair_norm, start_project, start_bias, residue_keys, start_output, H_Z)
    pair_one = (pairwise.astype(jnp.float32) + start_update).astype(jnp.bfloat16)
    rows_norm_one = layer_norm(pair_one)
    end_local = jnp.einsum(
        "kic,ch->hki", rows_norm_one, end_bias_map, preferred_element_type=jnp.float32
    ).astype(jnp.bfloat16)
    pair_cols, end_all = exchange_pair(pair_one, end_local, count)
    end_bias = jnp.swapaxes(end_all, 1, 2)
    column_norm = jnp.swapaxes(layer_norm(alignment_cols), 0, 1)
    column_update = attend(column_norm, column_project, None, sequence_keys, column_output, H_M)
    alignment_out = (alignment_cols.astype(jnp.float32) + jnp.swapaxes(column_update, 0, 1)).astype(
        jnp.bfloat16
    )
    end_norm = jnp.swapaxes(layer_norm(pair_cols), 0, 1)
    end_update = jnp.swapaxes(
        attend(end_norm, end_project, end_bias, residue_keys, end_output, H_Z), 0, 1
    )
    last_norm = layer_norm(alignment_out)
    weighting = sequence_mask.astype(jnp.float32)[:, None, None]
    left = (
        jnp.einsum("sic,co->sio", last_norm, outer_left, preferred_element_type=jnp.float32)
        * weighting
    ).astype(jnp.bfloat16)
    right = (
        jnp.einsum("sic,co->sio", last_norm, outer_right, preferred_element_type=jnp.float32)
        * weighting
    ).astype(jnp.bfloat16)
    row_count = jnp.sum(sequence_mask.astype(jnp.float32))
    left_all = lax.all_to_all(
        jnp.broadcast_to(left[None], (count,) + left.shape), "dap", 0, 0, tiled=True
    )
    outer_sum = (
        jnp.einsum("dsic,sje->dijce", left_all, right, preferred_element_type=jnp.float32)
        / row_count
    )
    outer_sum = outer_sum.reshape((-1,) + outer_sum.shape[2:])
    flattened = outer_sum.astype(jnp.bfloat16).reshape(outer_sum.shape[0], outer_sum.shape[1], -1)
    outer_update = jnp.einsum(
        "ijf,fc->ijc", flattened, outer_output, preferred_element_type=jnp.float32
    )
    pairwise_out = (pair_cols.astype(jnp.float32) + end_update + outer_update).astype(jnp.bfloat16)
    return (alignment_out, pairwise_out)


def solution(mesh):
    return jax.shard_map(
        functools.partial(per_device, count=mesh.shape["dap"]),
        mesh=mesh,
        in_specs=(
            P(("grp", "dap"), None, None),
            P(("grp", "dap"), None, None),
            P("grp"),
            P("grp"),
            P(),
            P(),
            P(),
            P(),
            P(),
            P(),
            P(),
            P(),
            P(),
            P(),
            P(),
            P(),
            P(),
            P(),
        ),
        out_specs=(P("grp", "dap", None), P("grp", "dap", None)),
        check_vma=False,
    )
```

```python
import functools

import jax
import jax.numpy as jnp
from jax import lax
from jax.sharding import PartitionSpec as P

H_M = 8
H_Z = 4


norm_epsilon = 1e-05
mask_scale = 1000000000.0


def layer_norm(values):
    widened = values.astype(jnp.float32)
    center = widened - jnp.mean(widened, axis=-1, keepdims=True)
    spread = jnp.mean(center * center, axis=-1, keepdims=True)
    return (center * lax.rsqrt(spread + norm_epsilon)).astype(jnp.bfloat16)


def key_offsets(mask_values):
    return (mask_values.astype(jnp.float32) - 1.0) * mask_scale


def project(inputs, weight_table):
    return jnp.einsum("bqc,cf->bqf", inputs, weight_table, preferred_element_type=jnp.float32)


def attend(inputs, weights, bias_table, key_bias, output_map, head_count):
    batch_size, query_count, width = inputs.shape
    query_all = project(inputs, weights[0]).astype(jnp.bfloat16)
    key_all = project(inputs, weights[1]).astype(jnp.bfloat16)
    value_all = project(inputs, weights[2]).astype(jnp.bfloat16)
    gating = jax.nn.sigmoid(project(inputs, weights[3]))
    head_size = query_all.shape[-1] // head_count
    query_heads = query_all.reshape(batch_size, query_count, head_count, head_size)
    key_heads = key_all.reshape(batch_size, query_count, head_count, head_size)
    value_heads = value_all.reshape(batch_size, query_count, head_count, head_size)
    scores = jnp.einsum(
        "bqhd,bkhd->bhqk", query_heads, key_heads, preferred_element_type=jnp.float32
    ) * head_size ** (-0.5)
    if bias_table is not None:
        scores = scores + bias_table.astype(jnp.float32)[None]
    scores = scores + key_bias
    softened = jax.nn.softmax(scores, axis=-1).astype(jnp.bfloat16)
    mixed = jnp.einsum("bhqk,bkhd->bqhd", softened, value_heads, preferred_element_type=jnp.float32)
    mixed = mixed.reshape(batch_size, query_count, head_count * head_size)
    gated = (mixed * gating).astype(jnp.bfloat16)
    return jnp.einsum("bqf,fc->bqc", gated, output_map, preferred_element_type=jnp.float32)


def gather_blocks(block, axis, count):
    spread = jnp.broadcast_to(block[None], (count,) + block.shape)
    received = lax.all_to_all(spread, "dap", 0, 0, tiled=True)
    received = jnp.moveaxis(received, 0, axis)
    shape = block.shape[:axis] + (count * block.shape[axis],) + block.shape[axis + 1 :]
    return received.reshape(shape)


def exchange_pair(pair_one, end_local, count):
    rows, width, channels = pair_one.shape
    block = width // count
    pair_part = jnp.moveaxis(pair_one.reshape(rows, count, block, channels), 1, 0)
    pair_part = pair_part.reshape(count, rows * block, channels)
    end_part = jnp.broadcast_to(
        end_local.reshape(1, -1, channels), (count, end_local.size // channels, channels)
    )
    received = lax.all_to_all(
        jnp.concatenate([pair_part, end_part], axis=1), "dap", 0, 0, tiled=True
    )
    pair_cols = received[:, : rows * block].reshape(count * rows, block, channels)
    end_all = received[:, rows * block :].reshape((count,) + end_local.shape)
    end_all = jnp.moveaxis(end_all, 0, 1).reshape(
        (end_local.shape[0], count * end_local.shape[1]) + end_local.shape[2:]
    )
    return pair_cols, end_all


def per_device(
    alignment,
    pairwise,
    sequence_mask,
    residue_mask,
    row_project,
    row_bias_map,
    row_output,
    column_project,
    column_output,
    start_project,
    start_bias_map,
    start_output,
    end_project,
    end_bias_map,
    end_output,
    outer_left,
    outer_right,
    outer_output,
    count=1,
):
    residue_keys = key_offsets(residue_mask)
    sequence_keys = key_offsets(sequence_mask)
    pair_norm = layer_norm(pairwise)
    both_maps = jnp.concatenate([row_bias_map, start_bias_map], axis=1)
    both_local = jnp.einsum(
        "ijc,ch->hij", pair_norm, both_maps, preferred_element_type=jnp.float32
    ).astype(jnp.bfloat16)
    both_bias = gather_blocks(both_local, 1, count)
    row_bias = both_bias[:H_M]
    start_bias = both_bias[H_M:]
    row_update = attend(layer_norm(alignment), row_project, row_bias, residue_keys, row_output, H_M)
    alignment_one = (alignment.astype(jnp.float32) + row_update).astype(jnp.bfloat16)
    alignment_cols = lax.all_to_all(alignment_one, "dap", 1, 0, tiled=True)
    start_update = attend(pair_norm, start_project, start_bias, residue_keys, start_output, H_Z)
    pair_one = (pairwise.astype(jnp.float32) + start_update).astype(jnp.bfloat16)
    rows_norm_one = layer_norm(pair_one)
    end_local = jnp.einsum(
        "kic,ch->hki", rows_norm_one, end_bias_map, preferred_element_type=jnp.float32
    ).astype(jnp.bfloat16)
    pair_cols, end_all = exchange_pair(pair_one, end_local, count)
    end_bias = jnp.swapaxes(end_all, 1, 2)
    column_norm = jnp.swapaxes(layer_norm(alignment_cols), 0, 1)
    column_update = attend(column_norm, column_project, None, sequence_keys, column_output, H_M)
    alignment_out = (alignment_cols.astype(jnp.float32) + jnp.swapaxes(column_update, 0, 1)).astype(
        jnp.bfloat16
    )
    end_norm = jnp.swapaxes(layer_norm(pair_cols), 0, 1)
    end_update = jnp.swapaxes(
        attend(end_norm, end_project, end_bias, residue_keys, end_output, H_Z), 0, 1
    )
    last_norm = layer_norm(alignment_out)
    weighting = sequence_mask.astype(jnp.float32)[:, None, None]
    left = (
        jnp.einsum("sic,co->sio", last_norm, outer_left, preferred_element_type=jnp.float32)
        * weighting
    ).astype(jnp.bfloat16)
    right = (
        jnp.einsum("sic,co->sio", last_norm, outer_right, preferred_element_type=jnp.float32)
        * weighting
    ).astype(jnp.bfloat16)
    row_count = jnp.sum(sequence_mask.astype(jnp.float32))
    outer_sum = (
        jnp.einsum(
            "sic,sje->ijce",
            gather_blocks(left, 1, count),
            right,
            preferred_element_type=jnp.float32,
        )
        / row_count
    )
    flattened = outer_sum.astype(jnp.bfloat16).reshape(outer_sum.shape[0], outer_sum.shape[1], -1)
    outer_update = jnp.einsum(
        "ijf,fc->ijc", flattened, outer_output, preferred_element_type=jnp.float32
    )
    pairwise_out = (pair_cols.astype(jnp.float32) + end_update + outer_update).astype(jnp.bfloat16)
    return (alignment_out, pairwise_out)


def solution(mesh):
    return jax.shard_map(
        functools.partial(per_device, count=mesh.shape["dap"]),
        mesh=mesh,
        in_specs=(
            P(("grp", "dap"), None, None),
            P(("grp", "dap"), None, None),
            P("grp"),
            P("grp"),
            P(),
            P(),
            P(),
            P(),
            P(),
            P(),
            P(),
            P(),
            P(),
            P(),
            P(),
            P(),
            P(),
            P(),
        ),
        out_specs=(P("grp", "dap", None), P("grp", "dap", None)),
        check_vma=False,
    )
```

```python
import functools

import jax
import jax.numpy as jnp
from jax import lax
from jax.sharding import PartitionSpec as P

H_M = 8
H_Z = 4
DAP = ("chip", "core")


norm_epsilon = 1e-05
mask_scale = 1000000000.0


def layer_norm(values):
    widened = values.astype(jnp.float32)
    center = widened - jnp.mean(widened, axis=-1, keepdims=True)
    spread = jnp.mean(center * center, axis=-1, keepdims=True)
    return (center * lax.rsqrt(spread + norm_epsilon)).astype(jnp.bfloat16)


def key_offsets(mask_values):
    return (mask_values.astype(jnp.float32) - 1.0) * mask_scale


def project(inputs, weight_table):
    return jnp.einsum("bqc,cf->bqf", inputs, weight_table, preferred_element_type=jnp.float32)


def attend(inputs, weights, bias_table, key_bias, output_map, head_count):
    batch_size, query_count, width = inputs.shape
    query_all = project(inputs, weights[0]).astype(jnp.bfloat16)
    key_all = project(inputs, weights[1]).astype(jnp.bfloat16)
    value_all = project(inputs, weights[2]).astype(jnp.bfloat16)
    gating = jax.nn.sigmoid(project(inputs, weights[3]))
    head_size = query_all.shape[-1] // head_count
    query_heads = query_all.reshape(batch_size, query_count, head_count, head_size)
    key_heads = key_all.reshape(batch_size, query_count, head_count, head_size)
    value_heads = value_all.reshape(batch_size, query_count, head_count, head_size)
    scores = jnp.einsum(
        "bqhd,bkhd->bhqk", query_heads, key_heads, preferred_element_type=jnp.float32
    ) * head_size ** (-0.5)
    if bias_table is not None:
        scores = scores + bias_table.astype(jnp.float32)[None]
    scores = scores + key_bias
    softened = jax.nn.softmax(scores, axis=-1).astype(jnp.bfloat16)
    mixed = jnp.einsum("bhqk,bkhd->bqhd", softened, value_heads, preferred_element_type=jnp.float32)
    mixed = mixed.reshape(batch_size, query_count, head_count * head_size)
    gated = (mixed * gating).astype(jnp.bfloat16)
    return jnp.einsum("bqf,fc->bqc", gated, output_map, preferred_element_type=jnp.float32)


def gather_blocks(block, axis, count):
    half = count // 2
    spread = jnp.broadcast_to(block[None], (half,) + block.shape)
    same_core = lax.all_to_all(spread, "chip", 0, 0, tiled=True)
    other_core = lax.ppermute(same_core, "core", [(0, 1), (1, 0)])
    first = lax.axis_index("core") == 0
    received = jnp.where(
        first,
        jnp.stack([same_core, other_core], axis=1),
        jnp.stack([other_core, same_core], axis=1),
    ).reshape((count,) + block.shape)
    received = jnp.moveaxis(received, 0, axis)
    shape = block.shape[:axis] + (count * block.shape[axis],) + block.shape[axis + 1 :]
    return received.reshape(shape)


def exchange_pair(pair_one, end_local, count):
    rows, width, channels = pair_one.shape
    block = width // count
    pair_part = jnp.moveaxis(pair_one.reshape(rows, count, block, channels), 1, 0)
    pair_part = pair_part.reshape(count, rows * block, channels)
    end_part = jnp.broadcast_to(
        end_local.reshape(1, -1, channels), (count, end_local.size // channels, channels)
    )
    received = lax.all_to_all(
        jnp.concatenate([pair_part, end_part], axis=1), DAP, 0, 0, tiled=True
    )
    pair_cols = received[:, : rows * block].reshape(count * rows, block, channels)
    end_all = received[:, rows * block :].reshape((count,) + end_local.shape)
    end_all = jnp.moveaxis(end_all, 0, 1).reshape(
        (end_local.shape[0], count * end_local.shape[1]) + end_local.shape[2:]
    )
    return pair_cols, end_all


def per_device(
    alignment,
    pairwise,
    sequence_mask,
    residue_mask,
    row_project,
    row_bias_map,
    row_output,
    column_project,
    column_output,
    start_project,
    start_bias_map,
    start_output,
    end_project,
    end_bias_map,
    end_output,
    outer_left,
    outer_right,
    outer_output,
    count=1,
):
    residue_keys = key_offsets(residue_mask)
    sequence_keys = key_offsets(sequence_mask)
    pair_norm = layer_norm(pairwise)
    both_maps = jnp.concatenate([row_bias_map, start_bias_map], axis=1)
    both_local = jnp.einsum(
        "ijc,ch->hij", pair_norm, both_maps, preferred_element_type=jnp.float32
    ).astype(jnp.bfloat16)
    both_bias = gather_blocks(both_local, 1, count)
    row_bias = both_bias[:H_M]
    start_bias = both_bias[H_M:]
    row_update = attend(layer_norm(alignment), row_project, row_bias, residue_keys, row_output, H_M)
    alignment_one = (alignment.astype(jnp.float32) + row_update).astype(jnp.bfloat16)
    alignment_cols = lax.all_to_all(alignment_one, DAP, 1, 0, tiled=True)
    start_update = attend(pair_norm, start_project, start_bias, residue_keys, start_output, H_Z)
    pair_one = (pairwise.astype(jnp.float32) + start_update).astype(jnp.bfloat16)
    rows_norm_one = layer_norm(pair_one)
    end_local = jnp.einsum(
        "kic,ch->hki", rows_norm_one, end_bias_map, preferred_element_type=jnp.float32
    ).astype(jnp.bfloat16)
    pair_cols, end_all = exchange_pair(pair_one, end_local, count)
    end_bias = jnp.swapaxes(end_all, 1, 2)
    column_norm = jnp.swapaxes(layer_norm(alignment_cols), 0, 1)
    column_update = attend(column_norm, column_project, None, sequence_keys, column_output, H_M)
    alignment_out = (alignment_cols.astype(jnp.float32) + jnp.swapaxes(column_update, 0, 1)).astype(
        jnp.bfloat16
    )
    end_norm = jnp.swapaxes(layer_norm(pair_cols), 0, 1)
    end_update = jnp.swapaxes(
        attend(end_norm, end_project, end_bias, residue_keys, end_output, H_Z), 0, 1
    )
    last_norm = layer_norm(alignment_out)
    weighting = sequence_mask.astype(jnp.float32)[:, None, None]
    left = (
        jnp.einsum("sic,co->sio", last_norm, outer_left, preferred_element_type=jnp.float32)
        * weighting
    ).astype(jnp.bfloat16)
    right = (
        jnp.einsum("sic,co->sio", last_norm, outer_right, preferred_element_type=jnp.float32)
        * weighting
    ).astype(jnp.bfloat16)
    row_count = jnp.sum(sequence_mask.astype(jnp.float32))
    outer_sum = (
        jnp.einsum(
            "sic,sje->ijce",
            gather_blocks(left, 1, count),
            right,
            preferred_element_type=jnp.float32,
        )
        / row_count
    )
    flattened = outer_sum.astype(jnp.bfloat16).reshape(outer_sum.shape[0], outer_sum.shape[1], -1)
    outer_update = jnp.einsum(
        "ijf,fc->ijc", flattened, outer_output, preferred_element_type=jnp.float32
    )
    pairwise_out = (pair_cols.astype(jnp.float32) + end_update + outer_update).astype(jnp.bfloat16)
    return (alignment_out, pairwise_out)


def solution(mesh):
    count = mesh.shape["dap"]
    split_mesh = jax.sharding.Mesh(
        mesh.devices.reshape(mesh.shape["grp"], count // 2, 2), ("grp",) + DAP
    )
    return jax.shard_map(
        functools.partial(per_device, count=count),
        mesh=split_mesh,
        in_specs=(
            P(("grp",) + DAP, None, None),
            P(("grp",) + DAP, None, None),
            P("grp"),
            P("grp"),
            P(),
            P(),
            P(),
            P(),
            P(),
            P(),
            P(),
            P(),
            P(),
            P(),
            P(),
            P(),
            P(),
            P(),
        ),
        out_specs=(P("grp", DAP, None), P("grp", DAP, None)),
        check_vma=False,
    )
```

```python
import functools

import jax
import jax.numpy as jnp
from jax import lax
from jax.sharding import PartitionSpec as P

H_M = 8
H_Z = 4
DAP = ("chip", "core")


norm_epsilon = 1e-05
mask_scale = 1000000000.0


def layer_norm(values):
    widened = values.astype(jnp.float32)
    center = widened - jnp.mean(widened, axis=-1, keepdims=True)
    spread = jnp.mean(center * center, axis=-1, keepdims=True)
    return (center * lax.rsqrt(spread + norm_epsilon)).astype(jnp.bfloat16)


def key_offsets(mask_values):
    return (mask_values.astype(jnp.float32) - 1.0) * mask_scale


def project(inputs, weight_table):
    return jnp.einsum("bqc,cf->bqf", inputs, weight_table, preferred_element_type=jnp.float32)


def attend(inputs, weights, bias_table, key_bias, output_map, head_count):
    batch_size, query_count, width = inputs.shape
    query_all = project(inputs, weights[0]).astype(jnp.bfloat16)
    key_all = project(inputs, weights[1]).astype(jnp.bfloat16)
    value_all = project(inputs, weights[2]).astype(jnp.bfloat16)
    gating = jax.nn.sigmoid(project(inputs, weights[3]))
    head_size = query_all.shape[-1] // head_count
    query_heads = query_all.reshape(batch_size, query_count, head_count, head_size)
    key_heads = key_all.reshape(batch_size, query_count, head_count, head_size)
    value_heads = value_all.reshape(batch_size, query_count, head_count, head_size)
    scores = jnp.einsum(
        "bqhd,bkhd->bhqk", query_heads, key_heads, preferred_element_type=jnp.float32
    ) * head_size ** (-0.5)
    if bias_table is not None:
        scores = scores + bias_table.astype(jnp.float32)[None]
    scores = scores + key_bias
    softened = jax.nn.softmax(scores, axis=-1).astype(jnp.bfloat16)
    mixed = jnp.einsum("bhqk,bkhd->bqhd", softened, value_heads, preferred_element_type=jnp.float32)
    mixed = mixed.reshape(batch_size, query_count, head_count * head_size)
    gated = (mixed * gating).astype(jnp.bfloat16)
    return jnp.einsum("bqf,fc->bqc", gated, output_map, preferred_element_type=jnp.float32)


def gather_blocks(block, axis, count):
    half = count // 2
    spread = jnp.broadcast_to(block[None], (half,) + block.shape)
    same_core = lax.all_to_all(spread, "chip", 0, 0, tiled=True)
    other_core = lax.ppermute(same_core, "core", [(0, 1), (1, 0)])
    first = lax.axis_index("core") == 0
    received = jnp.where(
        first,
        jnp.stack([same_core, other_core], axis=1),
        jnp.stack([other_core, same_core], axis=1),
    ).reshape((count,) + block.shape)
    received = jnp.moveaxis(received, 0, axis)
    shape = block.shape[:axis] + (count * block.shape[axis],) + block.shape[axis + 1 :]
    return received.reshape(shape)


def exchange_pair(pair_one, end_local, count):
    rows, width, channels = pair_one.shape
    block = width // count
    pair_part = jnp.moveaxis(pair_one.reshape(rows, count, block, channels), 1, 0)
    pair_part = pair_part.reshape(count, rows * block, channels)
    end_part = jnp.broadcast_to(
        end_local.reshape(1, -1, channels), (count, end_local.size // channels, channels)
    )
    received = lax.all_to_all(
        jnp.concatenate([pair_part, end_part], axis=1), DAP, 0, 0, tiled=True
    )
    pair_cols = received[:, : rows * block].reshape(count * rows, block, channels)
    end_all = received[:, rows * block :].reshape((count,) + end_local.shape)
    end_all = jnp.moveaxis(end_all, 0, 1).reshape(
        (end_local.shape[0], count * end_local.shape[1]) + end_local.shape[2:]
    )
    return pair_cols, end_all


def per_device(
    alignment,
    pairwise,
    sequence_mask,
    residue_mask,
    row_project,
    row_bias_map,
    row_output,
    column_project,
    column_output,
    start_project,
    start_bias_map,
    start_output,
    end_project,
    end_bias_map,
    end_output,
    outer_left,
    outer_right,
    outer_output,
    count=1,
):
    residue_keys = key_offsets(residue_mask)
    sequence_keys = key_offsets(sequence_mask)
    pair_norm = layer_norm(pairwise)
    both_maps = jnp.concatenate([row_bias_map, start_bias_map], axis=1)
    both_local = jnp.einsum(
        "ijc,ch->hij", pair_norm, both_maps, preferred_element_type=jnp.float32
    ).astype(jnp.bfloat16)
    both_bias = gather_blocks(both_local, 1, count)
    row_bias = both_bias[:H_M]
    start_bias = both_bias[H_M:]
    row_update = attend(layer_norm(alignment), row_project, row_bias, residue_keys, row_output, H_M)
    alignment_one = (alignment.astype(jnp.float32) + row_update).astype(jnp.bfloat16)
    alignment_cols = lax.all_to_all(alignment_one, DAP, 1, 0, tiled=True)
    start_update = attend(pair_norm, start_project, start_bias, residue_keys, start_output, H_Z)
    pair_one = (pairwise.astype(jnp.float32) + start_update).astype(jnp.bfloat16)
    rows_norm_one = layer_norm(pair_one)
    end_local = jnp.einsum(
        "kic,ch->hki", rows_norm_one, end_bias_map, preferred_element_type=jnp.float32
    ).astype(jnp.bfloat16)
    pair_cols, end_all = exchange_pair(pair_one, end_local, count)
    end_bias = jnp.swapaxes(end_all, 1, 2)
    column_norm = jnp.swapaxes(layer_norm(alignment_cols), 0, 1)
    column_update = attend(column_norm, column_project, None, sequence_keys, column_output, H_M)
    alignment_out = (alignment_cols.astype(jnp.float32) + jnp.swapaxes(column_update, 0, 1)).astype(
        jnp.bfloat16
    )
    end_norm = jnp.swapaxes(layer_norm(pair_cols), 0, 1)
    end_update = jnp.swapaxes(
        attend(end_norm, end_project, end_bias, residue_keys, end_output, H_Z), 0, 1
    )
    last_norm = layer_norm(alignment_out)
    weighting = sequence_mask.astype(jnp.float32)[:, None, None]
    left = (
        jnp.einsum("sic,co->ios", last_norm, outer_left, preferred_element_type=jnp.float32)
        * sequence_mask.astype(jnp.float32)
    ).astype(jnp.bfloat16)
    right = (
        jnp.einsum("sic,co->sio", last_norm, outer_right, preferred_element_type=jnp.float32)
        * weighting
    ).astype(jnp.bfloat16)
    row_count = jnp.sum(sequence_mask.astype(jnp.float32))
    outer_sum = (
        jnp.einsum(
            "ics,sje->ijce",
            gather_blocks(left, 0, count),
            right,
            preferred_element_type=jnp.float32,
        )
        / row_count
    )
    flattened = outer_sum.astype(jnp.bfloat16).reshape(outer_sum.shape[0], outer_sum.shape[1], -1)
    outer_update = jnp.einsum(
        "ijf,fc->ijc", flattened, outer_output, preferred_element_type=jnp.float32
    )
    pairwise_out = (pair_cols.astype(jnp.float32) + end_update + outer_update).astype(jnp.bfloat16)
    return (alignment_out, pairwise_out)


def solution(mesh):
    count = mesh.shape["dap"]
    split_mesh = jax.sharding.Mesh(
        mesh.devices.reshape(mesh.shape["grp"], count // 2, 2), ("grp",) + DAP
    )
    return jax.shard_map(
        functools.partial(per_device, count=count),
        mesh=split_mesh,
        in_specs=(
            P(("grp",) + DAP, None, None),
            P(("grp",) + DAP, None, None),
            P("grp"),
            P("grp"),
            P(),
            P(),
            P(),
            P(),
            P(),
            P(),
            P(),
            P(),
            P(),
            P(),
            P(),
            P(),
            P(),
            P(),
        ),
        out_specs=(P("grp", DAP, None), P("grp", DAP, None)),
        check_vma=False,
    )
```

```python
import functools

import jax
import jax.numpy as jnp
from jax import lax
from jax.sharding import PartitionSpec as P

H_M = 8
H_Z = 4
DAP = ("chip", "core")


norm_epsilon = 1e-05
mask_scale = 1000000000.0


def layer_norm(values):
    widened = values.astype(jnp.float32)
    center = widened - jnp.mean(widened, axis=-1, keepdims=True)
    spread = jnp.mean(center * center, axis=-1, keepdims=True)
    return (center * lax.rsqrt(spread + norm_epsilon)).astype(jnp.bfloat16)


def key_offsets(mask_values):
    return (mask_values.astype(jnp.float32) - 1.0) * mask_scale


def project(inputs, weight_table):
    return jnp.einsum("bqc,cf->bqf", inputs, weight_table, preferred_element_type=jnp.float32)


def attend(inputs, weights, bias_table, key_bias, output_map, head_count, order="bqc"):
    batch_size, query_count, width = inputs.shape
    query_all = project(inputs, weights[0]).astype(jnp.bfloat16)
    key_all = project(inputs, weights[1]).astype(jnp.bfloat16)
    value_all = project(inputs, weights[2]).astype(jnp.bfloat16)
    gating = jax.nn.sigmoid(project(inputs, weights[3]))
    head_size = query_all.shape[-1] // head_count
    query_heads = query_all.reshape(batch_size, query_count, head_count, head_size)
    key_heads = key_all.reshape(batch_size, query_count, head_count, head_size)
    value_heads = value_all.reshape(batch_size, query_count, head_count, head_size)
    scores = jnp.einsum(
        "bqhd,bkhd->bhqk", query_heads, key_heads, preferred_element_type=jnp.float32
    ) * head_size ** (-0.5)
    if bias_table is not None:
        scores = scores + bias_table.astype(jnp.float32)[None]
    scores = scores + key_bias
    softened = jax.nn.softmax(scores, axis=-1).astype(jnp.bfloat16)
    mixed = jnp.einsum("bhqk,bkhd->bqhd", softened, value_heads, preferred_element_type=jnp.float32)
    mixed = mixed.reshape(batch_size, query_count, head_count * head_size)
    gated = (mixed * gating).astype(jnp.bfloat16)
    return jnp.einsum("bqf,fc->" + order, gated, output_map, preferred_element_type=jnp.float32)


def gather_blocks(block, axis, count):
    half = count // 2
    spread = jnp.broadcast_to(block[None], (half,) + block.shape)
    same_core = lax.all_to_all(spread, "chip", 0, 0, tiled=True)
    other_core = lax.ppermute(same_core, "core", [(0, 1), (1, 0)])
    first = lax.axis_index("core") == 0
    received = jnp.where(
        first,
        jnp.stack([same_core, other_core], axis=1),
        jnp.stack([other_core, same_core], axis=1),
    ).reshape((count,) + block.shape)
    received = jnp.moveaxis(received, 0, axis)
    shape = block.shape[:axis] + (count * block.shape[axis],) + block.shape[axis + 1 :]
    return received.reshape(shape)


def exchange_pair(pair_one, end_local, count):
    rows, width, channels = pair_one.shape
    block = width // count
    pair_part = jnp.moveaxis(pair_one.reshape(rows, count, block, channels), 1, 0)
    pair_part = pair_part.reshape(count, rows * block, channels)
    end_part = jnp.broadcast_to(
        end_local.reshape(1, -1, channels), (count, end_local.size // channels, channels)
    )
    received = lax.all_to_all(
        jnp.concatenate([pair_part, end_part], axis=1), DAP, 0, 0, tiled=True
    )
    pair_cols = received[:, : rows * block].reshape(count * rows, block, channels)
    end_all = received[:, rows * block :].reshape((count,) + end_local.shape)
    end_all = jnp.moveaxis(end_all, 0, 1).reshape(
        (end_local.shape[0], count * end_local.shape[1]) + end_local.shape[2:]
    )
    return pair_cols, end_all


def per_device(
    alignment,
    pairwise,
    sequence_mask,
    residue_mask,
    row_project,
    row_bias_map,
    row_output,
    column_project,
    column_output,
    start_project,
    start_bias_map,
    start_output,
    end_project,
    end_bias_map,
    end_output,
    outer_left,
    outer_right,
    outer_output,
    count=1,
):
    residue_keys = key_offsets(residue_mask)
    sequence_keys = key_offsets(sequence_mask)
    pair_norm = layer_norm(pairwise)
    both_maps = jnp.concatenate([row_bias_map, start_bias_map], axis=1)
    both_local = jnp.einsum(
        "ijc,ch->hij", pair_norm, both_maps, preferred_element_type=jnp.float32
    ).astype(jnp.bfloat16)
    both_bias = gather_blocks(both_local, 1, count)
    row_bias = both_bias[:H_M]
    start_bias = both_bias[H_M:]
    row_update = attend(
        layer_norm(alignment), row_project, row_bias, residue_keys, row_output, H_M, "qbc"
    )
    alignment_one = (
        jnp.swapaxes(alignment, 0, 1).astype(jnp.float32) + row_update
    ).astype(jnp.bfloat16)
    alignment_one, start_bias = lax.optimization_barrier((alignment_one, start_bias))
    alignment_cols = lax.all_to_all(alignment_one, DAP, 0, 1, tiled=True)
    start_update = attend(pair_norm, start_project, start_bias, residue_keys, start_output, H_Z)
    pair_one = (pairwise.astype(jnp.float32) + start_update).astype(jnp.bfloat16)
    rows_norm_one = layer_norm(pair_one)
    end_local = jnp.einsum(
        "kic,ch->hki", rows_norm_one, end_bias_map, preferred_element_type=jnp.float32
    ).astype(jnp.bfloat16)
    pair_cols, end_all = exchange_pair(pair_one, end_local, count)
    end_bias = jnp.swapaxes(end_all, 1, 2)
    column_update = attend(
        layer_norm(alignment_cols), column_project, None, sequence_keys, column_output, H_M
    )
    alignment_turned = (alignment_cols.astype(jnp.float32) + column_update).astype(jnp.bfloat16)
    alignment_out = jnp.swapaxes(alignment_turned, 0, 1)
    end_norm = jnp.swapaxes(layer_norm(pair_cols), 0, 1)
    end_update = jnp.swapaxes(
        attend(end_norm, end_project, end_bias, residue_keys, end_output, H_Z), 0, 1
    )
    last_norm = layer_norm(alignment_turned)
    weighting = sequence_mask.astype(jnp.float32)[:, None, None]
    left = (
        jnp.einsum("isc,co->sio", last_norm, outer_left, preferred_element_type=jnp.float32)
        * weighting
    ).astype(jnp.bfloat16)
    right = (
        jnp.einsum("isc,co->sio", last_norm, outer_right, preferred_element_type=jnp.float32)
        * weighting
    ).astype(jnp.bfloat16)
    row_count = jnp.sum(sequence_mask.astype(jnp.float32))
    outer_sum = (
        jnp.einsum(
            "sic,sje->ijce",
            gather_blocks(left, 1, count),
            right,
            preferred_element_type=jnp.float32,
        )
        / row_count
    )
    flattened = outer_sum.astype(jnp.bfloat16).reshape(outer_sum.shape[0], outer_sum.shape[1], -1)
    outer_update = jnp.einsum(
        "ijf,fc->ijc", flattened, outer_output, preferred_element_type=jnp.float32
    )
    pairwise_out = (pair_cols.astype(jnp.float32) + end_update + outer_update).astype(jnp.bfloat16)
    return (alignment_out, pairwise_out)


def solution(mesh):
    count = mesh.shape["dap"]
    split_mesh = jax.sharding.Mesh(
        mesh.devices.reshape(mesh.shape["grp"], count // 2, 2), ("grp",) + DAP
    )
    return jax.shard_map(
        functools.partial(per_device, count=count),
        mesh=split_mesh,
        in_specs=(
            P(("grp",) + DAP, None, None),
            P(("grp",) + DAP, None, None),
            P("grp"),
            P("grp"),
            P(),
            P(),
            P(),
            P(),
            P(),
            P(),
            P(),
            P(),
            P(),
            P(),
            P(),
            P(),
            P(),
            P(),
        ),
        out_specs=(P("grp", DAP, None), P("grp", DAP, None)),
        check_vma=False,
    )
```

```python
import functools

import jax
import jax.numpy as jnp
from jax import lax
from jax.sharding import PartitionSpec as P

H_M = 8
H_Z = 4
DAP = ("chip", "core")


norm_epsilon = 1e-05
mask_scale = 1000000000.0


def layer_norm(values):
    widened = values.astype(jnp.float32)
    center = widened - jnp.mean(widened, axis=-1, keepdims=True)
    spread = jnp.mean(center * center, axis=-1, keepdims=True)
    return (center * lax.rsqrt(spread + norm_epsilon)).astype(jnp.bfloat16)


def key_offsets(mask_values):
    return (mask_values.astype(jnp.float32) - 1.0) * mask_scale


def project(inputs, weight_table):
    return jnp.einsum("bqc,cf->bqf", inputs, weight_table, preferred_element_type=jnp.float32)


def attend(inputs, weights, bias_table, key_bias, output_map, head_count):
    batch_size, query_count, width = inputs.shape
    query_all = project(inputs, weights[0]).astype(jnp.bfloat16)
    key_all = project(inputs, weights[1]).astype(jnp.bfloat16)
    value_all = project(inputs, weights[2]).astype(jnp.bfloat16)
    gating = jax.nn.sigmoid(project(inputs, weights[3]))
    head_size = query_all.shape[-1] // head_count
    query_heads = query_all.reshape(batch_size, query_count, head_count, head_size)
    key_heads = key_all.reshape(batch_size, query_count, head_count, head_size)
    value_heads = value_all.reshape(batch_size, query_count, head_count, head_size)
    scores = jnp.einsum(
        "bqhd,bkhd->bhqk", query_heads, key_heads, preferred_element_type=jnp.float32
    ) * head_size ** (-0.5)
    if bias_table is not None:
        scores = scores + bias_table.astype(jnp.float32)[None]
    scores = scores + key_bias
    softened = jax.nn.softmax(scores, axis=-1).astype(jnp.bfloat16)
    mixed = jnp.einsum("bhqk,bkhd->bqhd", softened, value_heads, preferred_element_type=jnp.float32)
    mixed = mixed.reshape(batch_size, query_count, head_count * head_size)
    gated = (mixed * gating).astype(jnp.bfloat16)
    return jnp.einsum("bqf,fc->bqc", gated, output_map, preferred_element_type=jnp.float32)


def gather_blocks(block, axis, count):
    half = count // 2
    spread = jnp.broadcast_to(block[None], (half,) + block.shape)
    same_core = lax.all_to_all(spread, "chip", 0, 0, tiled=True)
    other_core = lax.ppermute(same_core, "core", [(0, 1), (1, 0)])
    first = lax.axis_index("core") == 0
    received = jnp.where(
        first,
        jnp.stack([same_core, other_core], axis=1),
        jnp.stack([other_core, same_core], axis=1),
    ).reshape((count,) + block.shape)
    received = jnp.moveaxis(received, 0, axis)
    shape = block.shape[:axis] + (count * block.shape[axis],) + block.shape[axis + 1 :]
    return received.reshape(shape)


def exchange_pair(pair_one, end_local, count):
    rows, width, channels = pair_one.shape
    block = width // count
    pair_part = jnp.moveaxis(pair_one.reshape(rows, count, block, channels), 1, 0)
    pair_part = pair_part.reshape(count, rows * block, channels)
    end_part = jnp.broadcast_to(
        end_local.reshape(1, -1, channels), (count, end_local.size // channels, channels)
    )
    received = lax.all_to_all(
        jnp.concatenate([pair_part, end_part], axis=1), DAP, 0, 0, tiled=True
    )
    pair_cols = received[:, : rows * block].reshape(count * rows, block, channels)
    end_all = received[:, rows * block :].reshape((count,) + end_local.shape)
    end_all = jnp.moveaxis(end_all, 0, 1).reshape(
        (end_local.shape[0], count * end_local.shape[1]) + end_local.shape[2:]
    )
    return pair_cols, end_all


def per_device(
    alignment,
    pairwise,
    sequence_mask,
    residue_mask,
    row_project,
    row_bias_map,
    row_output,
    column_project,
    column_output,
    start_project,
    start_bias_map,
    start_output,
    end_project,
    end_bias_map,
    end_output,
    outer_left,
    outer_right,
    outer_output,
    count=1,
):
    residue_keys = key_offsets(residue_mask)
    sequence_keys = key_offsets(sequence_mask)
    both_maps = jnp.concatenate([row_bias_map, start_bias_map], axis=1)
    both_local = jnp.einsum(
        "ijc,ch->hij", layer_norm(pairwise), both_maps, preferred_element_type=jnp.float32
    ).astype(jnp.bfloat16)
    pair_norm = layer_norm(lax.optimization_barrier(pairwise))
    both_bias = gather_blocks(both_local, 1, count)
    row_bias = both_bias[:H_M]
    start_bias = both_bias[H_M:]
    row_update = attend(layer_norm(alignment), row_project, row_bias, residue_keys, row_output, H_M)
    alignment_one = (alignment.astype(jnp.float32) + row_update).astype(jnp.bfloat16)
    alignment_cols = lax.all_to_all(alignment_one, DAP, 1, 0, tiled=True)
    start_update = attend(pair_norm, start_project, start_bias, residue_keys, start_output, H_Z)
    pair_one = (pairwise.astype(jnp.float32) + start_update).astype(jnp.bfloat16)
    rows_norm_one = layer_norm(pair_one)
    end_local = jnp.einsum(
        "kic,ch->hki", rows_norm_one, end_bias_map, preferred_element_type=jnp.float32
    ).astype(jnp.bfloat16)
    pair_cols, end_all = exchange_pair(pair_one, end_local, count)
    end_bias = jnp.swapaxes(end_all, 1, 2)
    column_norm = jnp.swapaxes(layer_norm(alignment_cols), 0, 1)
    column_update = attend(column_norm, column_project, None, sequence_keys, column_output, H_M)
    alignment_out = (alignment_cols.astype(jnp.float32) + jnp.swapaxes(column_update, 0, 1)).astype(
        jnp.bfloat16
    )
    end_norm = jnp.swapaxes(layer_norm(pair_cols), 0, 1)
    end_update = jnp.swapaxes(
        attend(end_norm, end_project, end_bias, residue_keys, end_output, H_Z), 0, 1
    )
    last_norm = layer_norm(alignment_out)
    weighting = sequence_mask.astype(jnp.float32)[:, None, None]
    left = (
        jnp.einsum("sic,co->sio", last_norm, outer_left, preferred_element_type=jnp.float32)
        * weighting
    ).astype(jnp.bfloat16)
    right = (
        jnp.einsum("sic,co->sio", last_norm, outer_right, preferred_element_type=jnp.float32)
        * weighting
    ).astype(jnp.bfloat16)
    row_count = jnp.sum(sequence_mask.astype(jnp.float32))
    outer_sum = (
        jnp.einsum(
            "sic,sje->ijce",
            gather_blocks(left, 1, count),
            right,
            preferred_element_type=jnp.float32,
        )
        / row_count
    )
    flattened = outer_sum.astype(jnp.bfloat16).reshape(outer_sum.shape[0], outer_sum.shape[1], -1)
    outer_update = jnp.einsum(
        "ijf,fc->ijc", flattened, outer_output, preferred_element_type=jnp.float32
    )
    pairwise_out = (pair_cols.astype(jnp.float32) + end_update + outer_update).astype(jnp.bfloat16)
    return (alignment_out, pairwise_out)


def solution(mesh):
    count = mesh.shape["dap"]
    split_mesh = jax.sharding.Mesh(
        mesh.devices.reshape(mesh.shape["grp"], count // 2, 2), ("grp",) + DAP
    )
    return jax.shard_map(
        functools.partial(per_device, count=count),
        mesh=split_mesh,
        in_specs=(
            P(("grp",) + DAP, None, None),
            P(("grp",) + DAP, None, None),
            P("grp"),
            P("grp"),
            P(),
            P(),
            P(),
            P(),
            P(),
            P(),
            P(),
            P(),
            P(),
            P(),
            P(),
            P(),
            P(),
            P(),
        ),
        out_specs=(P("grp", DAP, None), P("grp", DAP, None)),
        check_vma=False,
    )
```

```python
import functools

import jax
import jax.numpy as jnp
from jax import lax
from jax.sharding import PartitionSpec as P

H_M = 8
H_Z = 4
DAP = ("chip", "core")


norm_epsilon = 1e-05
mask_scale = 1000000000.0


def layer_norm(values, axis=-1):
    widened = values.astype(jnp.float32)
    center = widened - jnp.mean(widened, axis=axis, keepdims=True)
    spread = jnp.mean(center * center, axis=axis, keepdims=True)
    return (center * lax.rsqrt(spread + norm_epsilon)).astype(jnp.bfloat16)


def key_offsets(mask_values):
    return (mask_values.astype(jnp.float32) - 1.0) * mask_scale


def project(inputs, weight_table):
    return jnp.einsum("bqc,cf->bqf", inputs, weight_table, preferred_element_type=jnp.float32)


def attend(inputs, weights, bias_table, key_bias, output_map, head_count):
    batch_size, query_count, width = inputs.shape
    query_all = project(inputs, weights[0]).astype(jnp.bfloat16)
    key_all = project(inputs, weights[1]).astype(jnp.bfloat16)
    value_all = project(inputs, weights[2]).astype(jnp.bfloat16)
    gating = jax.nn.sigmoid(project(inputs, weights[3]))
    head_size = query_all.shape[-1] // head_count
    query_heads = query_all.reshape(batch_size, query_count, head_count, head_size)
    key_heads = key_all.reshape(batch_size, query_count, head_count, head_size)
    value_heads = value_all.reshape(batch_size, query_count, head_count, head_size)
    scores = jnp.einsum(
        "bqhd,bkhd->bhqk", query_heads, key_heads, preferred_element_type=jnp.float32
    ) * head_size ** (-0.5)
    if bias_table is not None:
        scores = scores + bias_table.astype(jnp.float32)[None]
    scores = scores + key_bias
    softened = jax.nn.softmax(scores, axis=-1).astype(jnp.bfloat16)
    mixed = jnp.einsum("bhqk,bkhd->bqhd", softened, value_heads, preferred_element_type=jnp.float32)
    mixed = mixed.reshape(batch_size, query_count, head_count * head_size)
    gated = (mixed * gating).astype(jnp.bfloat16)
    return jnp.einsum("bqf,fc->bqc", gated, output_map, preferred_element_type=jnp.float32)


def gather_blocks(block, axis, count):
    half = count // 2
    spread = jnp.broadcast_to(block[None], (half,) + block.shape)
    same_core = lax.all_to_all(spread, "chip", 0, 0, tiled=True)
    other_core = lax.ppermute(same_core, "core", [(0, 1), (1, 0)])
    first = lax.axis_index("core") == 0
    received = jnp.where(
        first,
        jnp.stack([same_core, other_core], axis=1),
        jnp.stack([other_core, same_core], axis=1),
    ).reshape((count,) + block.shape)
    received = jnp.moveaxis(received, 0, axis)
    shape = block.shape[:axis] + (count * block.shape[axis],) + block.shape[axis + 1 :]
    return received.reshape(shape)


def exchange_pair(pair_one, end_local, count):
    rows, width, channels = pair_one.shape
    block = width // count
    pair_part = jnp.moveaxis(pair_one.reshape(rows, count, block, channels), 1, 0)
    pair_part = pair_part.reshape(count, rows * block, channels)
    end_part = jnp.broadcast_to(
        end_local.reshape(1, -1, channels), (count, end_local.size // channels, channels)
    )
    received = lax.all_to_all(
        jnp.concatenate([pair_part, end_part], axis=1), DAP, 0, 0, tiled=True
    )
    pair_cols = received[:, : rows * block].reshape(count * rows, block, channels)
    end_all = received[:, rows * block :].reshape((count,) + end_local.shape)
    end_all = jnp.moveaxis(end_all, 0, 1).reshape(
        (end_local.shape[0], count * end_local.shape[1]) + end_local.shape[2:]
    )
    return pair_cols, end_all


def per_device(
    alignment,
    pairwise,
    sequence_mask,
    residue_mask,
    row_project,
    row_bias_map,
    row_output,
    column_project,
    column_output,
    start_project,
    start_bias_map,
    start_output,
    end_project,
    end_bias_map,
    end_output,
    outer_left,
    outer_right,
    outer_output,
    count=1,
):
    residue_keys = key_offsets(residue_mask)
    sequence_keys = key_offsets(sequence_mask)
    both_maps = jnp.concatenate([row_bias_map, start_bias_map], axis=1)
    both_local = jnp.einsum(
        "icj,ch->hij",
        layer_norm(jnp.swapaxes(pairwise, 1, 2), axis=1),
        both_maps,
        preferred_element_type=jnp.float32,
    ).astype(jnp.bfloat16)
    pair_norm = layer_norm(lax.optimization_barrier(pairwise))
    both_bias = gather_blocks(both_local, 1, count)
    row_bias = both_bias[:H_M]
    start_bias = both_bias[H_M:]
    row_update = attend(layer_norm(alignment), row_project, row_bias, residue_keys, row_output, H_M)
    alignment_one = (alignment.astype(jnp.float32) + row_update).astype(jnp.bfloat16)
    alignment_cols = lax.all_to_all(alignment_one, DAP, 1, 0, tiled=True)
    start_update = attend(pair_norm, start_project, start_bias, residue_keys, start_output, H_Z)
    pair_one = (pairwise.astype(jnp.float32) + start_update).astype(jnp.bfloat16)
    rows_norm_one = layer_norm(pair_one)
    end_local = jnp.einsum(
        "kic,ch->hki", rows_norm_one, end_bias_map, preferred_element_type=jnp.float32
    ).astype(jnp.bfloat16)
    pair_cols, end_all = exchange_pair(pair_one, end_local, count)
    end_bias = jnp.swapaxes(end_all, 1, 2)
    column_norm = jnp.swapaxes(layer_norm(alignment_cols), 0, 1)
    column_update = attend(column_norm, column_project, None, sequence_keys, column_output, H_M)
    alignment_out = (alignment_cols.astype(jnp.float32) + jnp.swapaxes(column_update, 0, 1)).astype(
        jnp.bfloat16
    )
    end_norm = jnp.swapaxes(layer_norm(pair_cols), 0, 1)
    end_update = jnp.swapaxes(
        attend(end_norm, end_project, end_bias, residue_keys, end_output, H_Z), 0, 1
    )
    last_norm = layer_norm(alignment_out)
    weighting = sequence_mask.astype(jnp.float32)[:, None, None]
    left = (
        jnp.einsum("sic,co->sio", last_norm, outer_left, preferred_element_type=jnp.float32)
        * weighting
    ).astype(jnp.bfloat16)
    right = (
        jnp.einsum("sic,co->sio", last_norm, outer_right, preferred_element_type=jnp.float32)
        * weighting
    ).astype(jnp.bfloat16)
    row_count = jnp.sum(sequence_mask.astype(jnp.float32))
    outer_sum = (
        jnp.einsum(
            "sic,sje->ijce",
            gather_blocks(left, 1, count),
            right,
            preferred_element_type=jnp.float32,
        )
        / row_count
    )
    flattened = outer_sum.astype(jnp.bfloat16).reshape(outer_sum.shape[0], outer_sum.shape[1], -1)
    outer_update = jnp.einsum(
        "ijf,fc->ijc", flattened, outer_output, preferred_element_type=jnp.float32
    )
    pairwise_out = (pair_cols.astype(jnp.float32) + end_update + outer_update).astype(jnp.bfloat16)
    return (alignment_out, pairwise_out)


def solution(mesh):
    count = mesh.shape["dap"]
    split_mesh = jax.sharding.Mesh(
        mesh.devices.reshape(mesh.shape["grp"], count // 2, 2), ("grp",) + DAP
    )
    return jax.shard_map(
        functools.partial(per_device, count=count),
        mesh=split_mesh,
        in_specs=(
            P(("grp",) + DAP, None, None),
            P(("grp",) + DAP, None, None),
            P("grp"),
            P("grp"),
            P(),
            P(),
            P(),
            P(),
            P(),
            P(),
            P(),
            P(),
            P(),
            P(),
            P(),
            P(),
            P(),
            P(),
        ),
        out_specs=(P("grp", DAP, None), P("grp", DAP, None)),
        check_vma=False,
    )
```

```python
import functools

import jax
import jax.numpy as jnp
from jax import lax
from jax.sharding import PartitionSpec as P

H_M = 8
H_Z = 4
DAP = ("chip", "core")


norm_epsilon = 1e-05
mask_scale = 1000000000.0


def layer_norm(values, axis=-1):
    widened = values.astype(jnp.float32)
    center = widened - jnp.mean(widened, axis=axis, keepdims=True)
    spread = jnp.mean(center * center, axis=axis, keepdims=True)
    return (center * lax.rsqrt(spread + norm_epsilon)).astype(jnp.bfloat16)


def key_offsets(mask_values):
    return (mask_values.astype(jnp.float32) - 1.0) * mask_scale


def project(inputs, weight_table):
    return jnp.einsum("bqc,cf->bqf", inputs, weight_table, preferred_element_type=jnp.float32)


def attend(inputs, weights, bias_table, key_bias, output_map, head_count):
    batch_size, query_count, width = inputs.shape
    query_all = project(inputs, weights[0]).astype(jnp.bfloat16)
    key_all = project(inputs, weights[1]).astype(jnp.bfloat16)
    value_all = project(inputs, weights[2]).astype(jnp.bfloat16)
    gating = jax.nn.sigmoid(project(inputs, weights[3]))
    head_size = query_all.shape[-1] // head_count
    query_heads = query_all.reshape(batch_size, query_count, head_count, head_size)
    key_heads = key_all.reshape(batch_size, query_count, head_count, head_size)
    value_heads = value_all.reshape(batch_size, query_count, head_count, head_size)
    scores = jnp.einsum(
        "bqhd,bkhd->bhqk", query_heads, key_heads, preferred_element_type=jnp.float32
    ) * head_size ** (-0.5)
    if bias_table is not None:
        scores = scores + bias_table.astype(jnp.float32)[None]
    scores = scores + key_bias
    softened = jax.nn.softmax(scores, axis=-1).astype(jnp.bfloat16)
    mixed = jnp.einsum("bhqk,bkhd->bqhd", softened, value_heads, preferred_element_type=jnp.float32)
    mixed = mixed.reshape(batch_size, query_count, head_count * head_size)
    gated = (mixed * gating).astype(jnp.bfloat16)
    return jnp.einsum("bqf,fc->bqc", gated, output_map, preferred_element_type=jnp.float32)


def gather_blocks(block, axis, count):
    half = count // 2
    spread = jnp.broadcast_to(block[None], (half,) + block.shape)
    same_core = lax.all_to_all(spread, "chip", 0, 0, tiled=True)
    other_core = lax.ppermute(same_core, "core", [(0, 1), (1, 0)])
    first = lax.axis_index("core") == 0
    received = jnp.where(
        first,
        jnp.stack([same_core, other_core], axis=1),
        jnp.stack([other_core, same_core], axis=1),
    ).reshape((count,) + block.shape)
    received = jnp.moveaxis(received, 0, axis)
    shape = block.shape[:axis] + (count * block.shape[axis],) + block.shape[axis + 1 :]
    return received.reshape(shape)


def exchange_pair(pair_one, end_local, count):
    rows, width, channels = pair_one.shape
    block = width // count
    pair_part = jnp.moveaxis(pair_one.reshape(rows, count, block, channels), 1, 0)
    pair_part = pair_part.reshape(count, rows * block, channels)
    end_part = jnp.broadcast_to(
        end_local.reshape(1, -1, channels), (count, end_local.size // channels, channels)
    )
    received = lax.all_to_all(
        jnp.concatenate([pair_part, end_part], axis=1), DAP, 0, 0, tiled=True
    )
    pair_cols = received[:, : rows * block].reshape(count * rows, block, channels)
    end_all = received[:, rows * block :].reshape((count,) + end_local.shape)
    end_all = jnp.moveaxis(end_all, 0, 1).reshape(
        (end_local.shape[0], count * end_local.shape[1]) + end_local.shape[2:]
    )
    return pair_cols, end_all


def per_device(
    alignment,
    pairwise,
    sequence_mask,
    residue_mask,
    row_project,
    row_bias_map,
    row_output,
    column_project,
    column_output,
    start_project,
    start_bias_map,
    start_output,
    end_project,
    end_bias_map,
    end_output,
    outer_left,
    outer_right,
    outer_output,
    count=1,
):
    residue_keys = key_offsets(residue_mask)
    sequence_keys = key_offsets(sequence_mask)
    row_local = jnp.einsum(
        "icj,ch->hij",
        layer_norm(jnp.swapaxes(pairwise, 1, 2), axis=1),
        row_bias_map,
        preferred_element_type=jnp.float32,
    ).astype(jnp.bfloat16)
    row_bias = gather_blocks(row_local, 1, count)
    pair_norm = layer_norm(lax.optimization_barrier(pairwise))
    start_local = jnp.einsum(
        "ijc,ch->hij", pair_norm, start_bias_map, preferred_element_type=jnp.float32
    ).astype(jnp.bfloat16)
    start_bias = gather_blocks(start_local, 1, count)
    row_update = attend(layer_norm(alignment), row_project, row_bias, residue_keys, row_output, H_M)
    alignment_one = (alignment.astype(jnp.float32) + row_update).astype(jnp.bfloat16)
    alignment_cols = lax.all_to_all(alignment_one, DAP, 1, 0, tiled=True)
    start_update = attend(pair_norm, start_project, start_bias, residue_keys, start_output, H_Z)
    pair_one = (pairwise.astype(jnp.float32) + start_update).astype(jnp.bfloat16)
    rows_norm_one = layer_norm(pair_one)
    end_local = jnp.einsum(
        "kic,ch->hki", rows_norm_one, end_bias_map, preferred_element_type=jnp.float32
    ).astype(jnp.bfloat16)
    pair_cols, end_all = exchange_pair(pair_one, end_local, count)
    end_bias = jnp.swapaxes(end_all, 1, 2)
    column_norm = jnp.swapaxes(layer_norm(alignment_cols), 0, 1)
    column_update = attend(column_norm, column_project, None, sequence_keys, column_output, H_M)
    alignment_out = (alignment_cols.astype(jnp.float32) + jnp.swapaxes(column_update, 0, 1)).astype(
        jnp.bfloat16
    )
    end_norm = jnp.swapaxes(layer_norm(pair_cols), 0, 1)
    end_update = jnp.swapaxes(
        attend(end_norm, end_project, end_bias, residue_keys, end_output, H_Z), 0, 1
    )
    last_norm = layer_norm(alignment_out)
    weighting = sequence_mask.astype(jnp.float32)[:, None, None]
    left = (
        jnp.einsum("sic,co->sio", last_norm, outer_left, preferred_element_type=jnp.float32)
        * weighting
    ).astype(jnp.bfloat16)
    right = (
        jnp.einsum("sic,co->sio", last_norm, outer_right, preferred_element_type=jnp.float32)
        * weighting
    ).astype(jnp.bfloat16)
    row_count = jnp.sum(sequence_mask.astype(jnp.float32))
    outer_sum = (
        jnp.einsum(
            "sic,sje->ijce",
            gather_blocks(left, 1, count),
            right,
            preferred_element_type=jnp.float32,
        )
        / row_count
    )
    flattened = outer_sum.astype(jnp.bfloat16).reshape(outer_sum.shape[0], outer_sum.shape[1], -1)
    outer_update = jnp.einsum(
        "ijf,fc->ijc", flattened, outer_output, preferred_element_type=jnp.float32
    )
    pairwise_out = (pair_cols.astype(jnp.float32) + end_update + outer_update).astype(jnp.bfloat16)
    return (alignment_out, pairwise_out)


def solution(mesh):
    count = mesh.shape["dap"]
    split_mesh = jax.sharding.Mesh(
        mesh.devices.reshape(mesh.shape["grp"], count // 2, 2), ("grp",) + DAP
    )
    return jax.shard_map(
        functools.partial(per_device, count=count),
        mesh=split_mesh,
        in_specs=(
            P(("grp",) + DAP, None, None),
            P(("grp",) + DAP, None, None),
            P("grp"),
            P("grp"),
            P(),
            P(),
            P(),
            P(),
            P(),
            P(),
            P(),
            P(),
            P(),
            P(),
            P(),
            P(),
            P(),
            P(),
        ),
        out_specs=(P("grp", DAP, None), P("grp", DAP, None)),
        check_vma=False,
    )
```

```python
import functools

import jax
import jax.numpy as jnp
from jax import lax
from jax.sharding import PartitionSpec as P

H_M = 8
H_Z = 4
DAP = ("chip", "core")


norm_epsilon = 1e-05
mask_scale = 1000000000.0


def layer_norm(values):
    widened = values.astype(jnp.float32)
    center = widened - jnp.mean(widened, axis=-1, keepdims=True)
    spread = jnp.mean(center * center, axis=-1, keepdims=True)
    return (center * lax.rsqrt(spread + norm_epsilon)).astype(jnp.bfloat16)


def key_offsets(mask_values):
    return (mask_values.astype(jnp.float32) - 1.0) * mask_scale


def project(inputs, weight_table):
    return jnp.einsum("bqc,cf->bqf", inputs, weight_table, preferred_element_type=jnp.float32)


def attend(inputs, weights, bias_table, key_bias, output_map, head_count):
    batch_size, query_count, width = inputs.shape
    query_all = project(inputs, weights[0]).astype(jnp.bfloat16)
    key_all = project(inputs, weights[1]).astype(jnp.bfloat16)
    value_all = project(inputs, weights[2]).astype(jnp.bfloat16)
    gating = jax.nn.sigmoid(project(inputs, weights[3]))
    head_size = query_all.shape[-1] // head_count
    query_heads = query_all.reshape(batch_size, query_count, head_count, head_size)
    key_heads = key_all.reshape(batch_size, query_count, head_count, head_size)
    value_heads = value_all.reshape(batch_size, query_count, head_count, head_size)
    scores = jnp.einsum(
        "bqhd,bkhd->bhqk", query_heads, key_heads, preferred_element_type=jnp.float32
    ) * head_size ** (-0.5)
    if bias_table is not None:
        scores = scores + bias_table.astype(jnp.float32)[None]
    scores = scores + key_bias
    softened = jax.nn.softmax(scores, axis=-1).astype(jnp.bfloat16)
    mixed = jnp.einsum("bhqk,bkhd->bqhd", softened, value_heads, preferred_element_type=jnp.float32)
    mixed = mixed.reshape(batch_size, query_count, head_count * head_size)
    gated = (mixed * gating).astype(jnp.bfloat16)
    return jnp.einsum("bqf,fc->bqc", gated, output_map, preferred_element_type=jnp.float32)


def gather_blocks(block, axis, count):
    half = count // 2
    spread = jnp.broadcast_to(block[None], (half,) + block.shape)
    same_core = lax.all_to_all(spread, "chip", 0, 0, tiled=True)
    other_core = lax.ppermute(same_core, "core", [(0, 1), (1, 0)])
    first = lax.axis_index("core") == 0
    received = jnp.where(
        first,
        jnp.stack([same_core, other_core], axis=1),
        jnp.stack([other_core, same_core], axis=1),
    ).reshape((count,) + block.shape)
    received = jnp.moveaxis(received, 0, axis)
    shape = block.shape[:axis] + (count * block.shape[axis],) + block.shape[axis + 1 :]
    return received.reshape(shape)


def exchange_pair(pair_one, end_local, count):
    rows, width, channels = pair_one.shape
    block = width // count
    pair_part = jnp.moveaxis(pair_one.reshape(rows, count, block, channels), 1, 0)
    pair_part = pair_part.reshape(count, rows * block, channels)
    end_part = jnp.broadcast_to(
        end_local.reshape(1, -1, channels), (count, end_local.size // channels, channels)
    )
    received = lax.all_to_all(
        jnp.concatenate([pair_part, end_part], axis=1), DAP, 0, 0, tiled=True
    )
    pair_cols = received[:, : rows * block].reshape(count * rows, block, channels)
    end_all = received[:, rows * block :].reshape((count,) + end_local.shape)
    end_all = jnp.moveaxis(end_all, 0, 1).reshape(
        (end_local.shape[0], count * end_local.shape[1]) + end_local.shape[2:]
    )
    return pair_cols, end_all


def per_device(
    alignment,
    pairwise,
    sequence_mask,
    residue_mask,
    row_project,
    row_bias_map,
    row_output,
    column_project,
    column_output,
    start_project,
    start_bias_map,
    start_output,
    end_project,
    end_bias_map,
    end_output,
    outer_left,
    outer_right,
    outer_output,
    count=1,
):
    residue_keys = key_offsets(residue_mask)
    sequence_keys = key_offsets(sequence_mask)
    pair_norm = layer_norm(pairwise)
    both_maps = jnp.concatenate([row_bias_map, start_bias_map], axis=1)
    both_local = jnp.einsum(
        "ijc,ch->hij", pair_norm, both_maps, preferred_element_type=jnp.float32
    ).astype(jnp.bfloat16)
    both_bias = gather_blocks(both_local, 1, count)
    row_bias = both_bias[:H_M]
    start_bias = both_bias[H_M:]
    row_update = attend(layer_norm(alignment), row_project, row_bias, residue_keys, row_output, H_M)
    alignment_one = (alignment.astype(jnp.float32) + row_update).astype(jnp.bfloat16)
    alignment_cols = lax.all_to_all(alignment_one, DAP, 1, 0, tiled=True)
    start_update = attend(pair_norm, start_project, start_bias, residue_keys, start_output, H_Z)
    pair_one = (pairwise.astype(jnp.float32) + start_update).astype(jnp.bfloat16)
    rows_norm_one = layer_norm(pair_one)
    end_local = jnp.einsum(
        "kic,ch->hki", rows_norm_one, end_bias_map, preferred_element_type=jnp.float32
    ).astype(jnp.bfloat16)
    pair_cols, end_all = exchange_pair(pair_one, end_local, count)
    end_bias = jnp.swapaxes(end_all, 1, 2)
    column_norm = jnp.swapaxes(layer_norm(alignment_cols), 0, 1)
    column_update = attend(column_norm, column_project, None, sequence_keys, column_output, H_M)
    alignment_out = (alignment_cols.astype(jnp.float32) + jnp.swapaxes(column_update, 0, 1)).astype(
        jnp.bfloat16
    )
    end_norm = jnp.swapaxes(layer_norm(pair_cols), 0, 1)
    end_update = jnp.swapaxes(
        attend(end_norm, end_project, end_bias, residue_keys, end_output, H_Z), 0, 1
    )
    last_norm = layer_norm(alignment_out)
    weighting = sequence_mask.astype(jnp.float32)[:, None, None]
    left = (
        jnp.einsum("sic,co->sio", last_norm, outer_left, preferred_element_type=jnp.float32)
        * weighting
    ).astype(jnp.bfloat16)
    right = (
        jnp.einsum("sic,co->sio", last_norm, outer_right, preferred_element_type=jnp.float32)
        * weighting
    ).astype(jnp.bfloat16)
    row_count = jnp.sum(sequence_mask.astype(jnp.float32))
    half = count // 2
    same_core = lax.all_to_all(
        jnp.broadcast_to(left[None], (half,) + left.shape), "chip", 0, 0, tiled=True
    )
    other_core = lax.ppermute(same_core, "core", [(0, 1), (1, 0)])

    def outer_rows(received):
        gathered = jnp.moveaxis(received, 0, 1).reshape(
            left.shape[0], half * left.shape[1], left.shape[2]
        )
        outer_sum = (
            jnp.einsum("sic,sje->ijce", gathered, right, preferred_element_type=jnp.float32)
            / row_count
        )
        flattened = outer_sum.astype(jnp.bfloat16).reshape(
            outer_sum.shape[0], outer_sum.shape[1], -1
        )
        rows = jnp.einsum("ijf,fc->ijc", flattened, outer_output, preferred_element_type=jnp.float32)
        return rows.reshape((half, left.shape[1]) + rows.shape[1:])

    own_rows = outer_rows(same_core)
    partner_rows = outer_rows(other_core)
    first = lax.axis_index("core") == 0
    outer_update = jnp.where(
        first,
        jnp.stack([own_rows, partner_rows], axis=1),
        jnp.stack([partner_rows, own_rows], axis=1),
    ).reshape(pair_cols.shape)
    pairwise_out = (pair_cols.astype(jnp.float32) + end_update + outer_update).astype(jnp.bfloat16)
    return (alignment_out, pairwise_out)


def solution(mesh):
    count = mesh.shape["dap"]
    split_mesh = jax.sharding.Mesh(
        mesh.devices.reshape(mesh.shape["grp"], count // 2, 2), ("grp",) + DAP
    )
    return jax.shard_map(
        functools.partial(per_device, count=count),
        mesh=split_mesh,
        in_specs=(
            P(("grp",) + DAP, None, None),
            P(("grp",) + DAP, None, None),
            P("grp"),
            P("grp"),
            P(),
            P(),
            P(),
            P(),
            P(),
            P(),
            P(),
            P(),
            P(),
            P(),
            P(),
            P(),
            P(),
            P(),
        ),
        out_specs=(P("grp", DAP, None), P("grp", DAP, None)),
        check_vma=False,
    )
```

```python
import functools

import jax
import jax.numpy as jnp
from jax import lax
from jax.sharding import PartitionSpec as P

H_M = 8
H_Z = 4
DAP = ("chip", "core")


norm_epsilon = 1e-05
mask_scale = 1000000000.0


def layer_norm(values):
    widened = values.astype(jnp.float32)
    center = widened - jnp.mean(widened, axis=-1, keepdims=True)
    spread = jnp.mean(center * center, axis=-1, keepdims=True)
    return (center * lax.rsqrt(spread + norm_epsilon)).astype(jnp.bfloat16)


def key_offsets(mask_values):
    return (mask_values.astype(jnp.float32) - 1.0) * mask_scale


def project(inputs, weight_table):
    return jnp.einsum("bqc,cf->bqf", inputs, weight_table, preferred_element_type=jnp.float32)


def attend(inputs, weights, bias_table, key_bias, output_map, head_count):
    batch_size, query_count, width = inputs.shape
    query_all = project(inputs, weights[0]).astype(jnp.bfloat16)
    key_all = project(inputs, weights[1]).astype(jnp.bfloat16)
    value_all = project(inputs, weights[2]).astype(jnp.bfloat16)
    gating = jax.nn.sigmoid(project(inputs, weights[3]))
    head_size = query_all.shape[-1] // head_count
    query_heads = query_all.reshape(batch_size, query_count, head_count, head_size)
    key_heads = key_all.reshape(batch_size, query_count, head_count, head_size)
    value_heads = value_all.reshape(batch_size, query_count, head_count, head_size)
    scores = jnp.einsum(
        "bqhd,bkhd->bhqk", query_heads, key_heads, preferred_element_type=jnp.float32
    ) * head_size ** (-0.5)
    if bias_table is not None:
        scores = scores + bias_table.astype(jnp.float32)[None]
    scores = scores + key_bias
    softened = jax.nn.softmax(scores, axis=-1).astype(jnp.bfloat16)
    mixed = jnp.einsum("bhqk,bkhd->bqhd", softened, value_heads, preferred_element_type=jnp.float32)
    mixed = mixed.reshape(batch_size, query_count, head_count * head_size)
    gated = (mixed * gating).astype(jnp.bfloat16)
    return jnp.einsum("bqf,fc->bqc", gated, output_map, preferred_element_type=jnp.float32)


def gather_spread(spread, axis, count):
    same_core = lax.all_to_all(spread, "chip", 0, 0, tiled=True)
    other_core = lax.ppermute(same_core, "core", [(0, 1), (1, 0)])
    first = lax.axis_index("core") == 0
    block = spread.shape[1:]
    received = jnp.where(
        first,
        jnp.stack([same_core, other_core], axis=1),
        jnp.stack([other_core, same_core], axis=1),
    ).reshape((count,) + block)
    received = jnp.moveaxis(received, 0, axis)
    shape = block[:axis] + (count * block[axis],) + block[axis + 1 :]
    return received.reshape(shape)


def spread_maps(maps, count):
    return jnp.broadcast_to(maps[None], (count // 2,) + maps.shape)


def exchange_pair(pair_one, end_local, count):
    rows, width, channels = pair_one.shape
    block = width // count
    pair_part = jnp.moveaxis(pair_one.reshape(rows, count, block, channels), 1, 0)
    pair_part = pair_part.reshape(count, rows * block, channels)
    end_part = jnp.broadcast_to(
        end_local.reshape(1, -1, channels), (count, end_local.size // channels, channels)
    )
    received = lax.all_to_all(
        jnp.concatenate([pair_part, end_part], axis=1), DAP, 0, 0, tiled=True
    )
    pair_cols = received[:, : rows * block].reshape(count * rows, block, channels)
    end_all = received[:, rows * block :].reshape((count,) + end_local.shape)
    end_all = jnp.moveaxis(end_all, 0, 1).reshape(
        (end_local.shape[0], count * end_local.shape[1]) + end_local.shape[2:]
    )
    return pair_cols, end_all


def per_device(
    alignment,
    pairwise,
    sequence_mask,
    residue_mask,
    row_project,
    row_bias_map,
    row_output,
    column_project,
    column_output,
    start_project,
    start_bias_map,
    start_output,
    end_project,
    end_bias_map,
    end_output,
    outer_left,
    outer_right,
    outer_output,
    count=1,
):
    residue_keys = key_offsets(residue_mask)
    sequence_keys = key_offsets(sequence_mask)
    pair_norm = layer_norm(pairwise)
    both_maps = jnp.concatenate([row_bias_map, start_bias_map], axis=1)
    both_spread = jnp.einsum(
        "ijc,dch->dhij", pair_norm, spread_maps(both_maps, count), preferred_element_type=jnp.float32
    ).astype(jnp.bfloat16)
    both_bias = gather_spread(both_spread, 1, count)
    row_bias = both_bias[:H_M]
    start_bias = both_bias[H_M:]
    row_update = attend(layer_norm(alignment), row_project, row_bias, residue_keys, row_output, H_M)
    alignment_one = (alignment.astype(jnp.float32) + row_update).astype(jnp.bfloat16)
    alignment_cols = lax.all_to_all(alignment_one, DAP, 1, 0, tiled=True)
    start_update = attend(pair_norm, start_project, start_bias, residue_keys, start_output, H_Z)
    pair_one = (pairwise.astype(jnp.float32) + start_update).astype(jnp.bfloat16)
    rows_norm_one = layer_norm(pair_one)
    end_local = jnp.einsum(
        "kic,ch->hki", rows_norm_one, end_bias_map, preferred_element_type=jnp.float32
    ).astype(jnp.bfloat16)
    pair_cols, end_all = exchange_pair(pair_one, end_local, count)
    end_bias = jnp.swapaxes(end_all, 1, 2)
    column_norm = jnp.swapaxes(layer_norm(alignment_cols), 0, 1)
    column_update = attend(column_norm, column_project, None, sequence_keys, column_output, H_M)
    alignment_out = (alignment_cols.astype(jnp.float32) + jnp.swapaxes(column_update, 0, 1)).astype(
        jnp.bfloat16
    )
    end_norm = jnp.swapaxes(layer_norm(pair_cols), 0, 1)
    end_update = jnp.swapaxes(
        attend(end_norm, end_project, end_bias, residue_keys, end_output, H_Z), 0, 1
    )
    last_norm = layer_norm(alignment_out)
    weighting = sequence_mask.astype(jnp.float32)[:, None, None]
    left_spread = (
        jnp.einsum(
            "sic,dco->dsio", last_norm, spread_maps(outer_left, count), preferred_element_type=jnp.float32
        )
        * weighting
    ).astype(jnp.bfloat16)
    right = (
        jnp.einsum("sic,co->sio", last_norm, outer_right, preferred_element_type=jnp.float32)
        * weighting
    ).astype(jnp.bfloat16)
    row_count = jnp.sum(sequence_mask.astype(jnp.float32))
    outer_sum = (
        jnp.einsum(
            "sic,sje->ijce",
            gather_spread(left_spread, 1, count),
            right,
            preferred_element_type=jnp.float32,
        )
        / row_count
    )
    flattened = outer_sum.astype(jnp.bfloat16).reshape(outer_sum.shape[0], outer_sum.shape[1], -1)
    outer_update = jnp.einsum(
        "ijf,fc->ijc", flattened, outer_output, preferred_element_type=jnp.float32
    )
    pairwise_out = (pair_cols.astype(jnp.float32) + end_update + outer_update).astype(jnp.bfloat16)
    return (alignment_out, pairwise_out)


def solution(mesh):
    count = mesh.shape["dap"]
    split_mesh = jax.sharding.Mesh(
        mesh.devices.reshape(mesh.shape["grp"], count // 2, 2), ("grp",) + DAP
    )
    return jax.shard_map(
        functools.partial(per_device, count=count),
        mesh=split_mesh,
        in_specs=(
            P(("grp",) + DAP, None, None),
            P(("grp",) + DAP, None, None),
            P("grp"),
            P("grp"),
            P(),
            P(),
            P(),
            P(),
            P(),
            P(),
            P(),
            P(),
            P(),
            P(),
            P(),
            P(),
            P(),
            P(),
        ),
        out_specs=(P("grp", DAP, None), P("grp", DAP, None)),
        check_vma=False,
    )
```

```python
import functools

import jax
import jax.numpy as jnp
from jax import lax
from jax.sharding import PartitionSpec as P

H_M = 8
H_Z = 4
DAP = ("chip", "core")


norm_epsilon = 1e-05
mask_scale = 1000000000.0


def layer_norm(values):
    widened = values.astype(jnp.float32)
    center = widened - jnp.mean(widened, axis=-1, keepdims=True)
    spread = jnp.mean(center * center, axis=-1, keepdims=True)
    return (center * lax.rsqrt(spread + norm_epsilon)).astype(jnp.bfloat16)


def key_offsets(mask_values):
    return (mask_values.astype(jnp.float32) - 1.0) * mask_scale


def project(inputs, weight_table):
    return jnp.einsum("bqc,cf->bqf", inputs, weight_table, preferred_element_type=jnp.float32)


def attend(inputs, weights, bias_table, key_bias, output_map, head_count):
    batch_size, query_count, width = inputs.shape
    query_all = project(inputs, weights[0]).astype(jnp.bfloat16)
    key_all = project(inputs, weights[1]).astype(jnp.bfloat16)
    value_all = project(inputs, weights[2]).astype(jnp.bfloat16)
    gating = jax.nn.sigmoid(project(inputs, weights[3]))
    head_size = query_all.shape[-1] // head_count
    query_heads = query_all.reshape(batch_size, query_count, head_count, head_size)
    key_heads = key_all.reshape(batch_size, query_count, head_count, head_size)
    value_heads = value_all.reshape(batch_size, query_count, head_count, head_size)
    scores = jnp.einsum(
        "bqhd,bkhd->bhqk", query_heads, key_heads, preferred_element_type=jnp.float32
    ) * head_size ** (-0.5)
    if bias_table is not None:
        scores = scores + bias_table.astype(jnp.float32)[None]
    scores = scores + key_bias
    softened = jax.nn.softmax(scores, axis=-1).astype(jnp.bfloat16)
    mixed = jnp.einsum("bhqk,bkhd->bqhd", softened, value_heads, preferred_element_type=jnp.float32)
    mixed = mixed.reshape(batch_size, query_count, head_count * head_size)
    gated = (mixed * gating).astype(jnp.bfloat16)
    return jnp.einsum("bqf,fc->bqc", gated, output_map, preferred_element_type=jnp.float32)


def gather_blocks(block, axis, count):
    half = count // 2
    spread = jnp.broadcast_to(block[None], (half,) + block.shape)
    same_core = lax.all_to_all(spread, "chip", 0, 0, tiled=True)
    other_core = lax.ppermute(same_core, "core", [(0, 1), (1, 0)])
    both = jnp.stack([other_core, same_core, other_core], axis=1)
    received = lax.dynamic_slice_in_dim(both, 1 - lax.axis_index("core"), 2, axis=1)
    received = received.reshape((count,) + block.shape)
    received = jnp.moveaxis(received, 0, axis)
    shape = block.shape[:axis] + (count * block.shape[axis],) + block.shape[axis + 1 :]
    return received.reshape(shape)


def exchange_pair(pair_one, end_local, count):
    rows, width, channels = pair_one.shape
    block = width // count
    pair_part = jnp.moveaxis(pair_one.reshape(rows, count, block, channels), 1, 0)
    pair_part = pair_part.reshape(count, rows * block, channels)
    end_part = jnp.broadcast_to(
        end_local.reshape(1, -1, channels), (count, end_local.size // channels, channels)
    )
    received = lax.all_to_all(
        jnp.concatenate([pair_part, end_part], axis=1), DAP, 0, 0, tiled=True
    )
    pair_cols = received[:, : rows * block].reshape(count * rows, block, channels)
    end_all = received[:, rows * block :].reshape((count,) + end_local.shape)
    end_all = jnp.moveaxis(end_all, 0, 1).reshape(
        (end_local.shape[0], count * end_local.shape[1]) + end_local.shape[2:]
    )
    return pair_cols, end_all


def per_device(
    alignment,
    pairwise,
    sequence_mask,
    residue_mask,
    row_project,
    row_bias_map,
    row_output,
    column_project,
    column_output,
    start_project,
    start_bias_map,
    start_output,
    end_project,
    end_bias_map,
    end_output,
    outer_left,
    outer_right,
    outer_output,
    count=1,
):
    residue_keys = key_offsets(residue_mask)
    sequence_keys = key_offsets(sequence_mask)
    pair_norm = layer_norm(pairwise)
    both_maps = jnp.concatenate([row_bias_map, start_bias_map], axis=1)
    both_local = jnp.einsum(
        "ijc,ch->hij", pair_norm, both_maps, preferred_element_type=jnp.float32
    ).astype(jnp.bfloat16)
    both_bias = gather_blocks(both_local, 1, count)
    row_bias = both_bias[:H_M]
    start_bias = both_bias[H_M:]
    row_update = attend(layer_norm(alignment), row_project, row_bias, residue_keys, row_output, H_M)
    alignment_one = (alignment.astype(jnp.float32) + row_update).astype(jnp.bfloat16)
    alignment_cols = lax.all_to_all(alignment_one, DAP, 1, 0, tiled=True)
    start_update = attend(pair_norm, start_project, start_bias, residue_keys, start_output, H_Z)
    pair_one = (pairwise.astype(jnp.float32) + start_update).astype(jnp.bfloat16)
    rows_norm_one = layer_norm(pair_one)
    end_local = jnp.einsum(
        "kic,ch->hki", rows_norm_one, end_bias_map, preferred_element_type=jnp.float32
    ).astype(jnp.bfloat16)
    pair_cols, end_all = exchange_pair(pair_one, end_local, count)
    end_bias = jnp.swapaxes(end_all, 1, 2)
    column_norm = jnp.swapaxes(layer_norm(alignment_cols), 0, 1)
    column_update = attend(column_norm, column_project, None, sequence_keys, column_output, H_M)
    alignment_out = (alignment_cols.astype(jnp.float32) + jnp.swapaxes(column_update, 0, 1)).astype(
        jnp.bfloat16
    )
    end_norm = jnp.swapaxes(layer_norm(pair_cols), 0, 1)
    end_update = jnp.swapaxes(
        attend(end_norm, end_project, end_bias, residue_keys, end_output, H_Z), 0, 1
    )
    last_norm = layer_norm(alignment_out)
    weighting = sequence_mask.astype(jnp.float32)[:, None, None]
    left = (
        jnp.einsum("sic,co->sio", last_norm, outer_left, preferred_element_type=jnp.float32)
        * weighting
    ).astype(jnp.bfloat16)
    right = (
        jnp.einsum("sic,co->sio", last_norm, outer_right, preferred_element_type=jnp.float32)
        * weighting
    ).astype(jnp.bfloat16)
    row_count = jnp.sum(sequence_mask.astype(jnp.float32))
    outer_sum = (
        jnp.einsum(
            "sic,sje->ijce",
            gather_blocks(left, 1, count),
            right,
            preferred_element_type=jnp.float32,
        )
        / row_count
    )
    flattened = outer_sum.astype(jnp.bfloat16).reshape(outer_sum.shape[0], outer_sum.shape[1], -1)
    outer_update = jnp.einsum(
        "ijf,fc->ijc", flattened, outer_output, preferred_element_type=jnp.float32
    )
    pairwise_out = (pair_cols.astype(jnp.float32) + end_update + outer_update).astype(jnp.bfloat16)
    return (alignment_out, pairwise_out)


def solution(mesh):
    count = mesh.shape["dap"]
    split_mesh = jax.sharding.Mesh(
        mesh.devices.reshape(mesh.shape["grp"], count // 2, 2), ("grp",) + DAP
    )
    return jax.shard_map(
        functools.partial(per_device, count=count),
        mesh=split_mesh,
        in_specs=(
            P(("grp",) + DAP, None, None),
            P(("grp",) + DAP, None, None),
            P("grp"),
            P("grp"),
            P(),
            P(),
            P(),
            P(),
            P(),
            P(),
            P(),
            P(),
            P(),
            P(),
            P(),
            P(),
            P(),
            P(),
        ),
        out_specs=(P("grp", DAP, None), P("grp", DAP, None)),
        check_vma=False,
    )
```

```python
import functools

import jax
import jax.numpy as jnp
from jax import lax
from jax.sharding import PartitionSpec as P

H_M = 8
H_Z = 4
DAP = ("chip", "core")


norm_epsilon = 1e-05
mask_scale = 1000000000.0


def layer_norm(values):
    widened = values.astype(jnp.float32)
    center = widened - jnp.mean(widened, axis=-1, keepdims=True)
    spread = jnp.mean(center * center, axis=-1, keepdims=True)
    return (center * lax.rsqrt(spread + norm_epsilon)).astype(jnp.bfloat16)


def key_offsets(mask_values):
    return (mask_values.astype(jnp.float32) - 1.0) * mask_scale


def project(inputs, weight_table):
    return jnp.einsum("bqc,cf->bqf", inputs, weight_table, preferred_element_type=jnp.float32)


def attend(inputs, weights, bias_table, key_bias, output_map, head_count, early=False):
    batch_size, query_count, width = inputs.shape
    query_all = project(inputs, weights[0]).astype(jnp.bfloat16)
    key_all = project(inputs, weights[1]).astype(jnp.bfloat16)
    value_all = project(inputs, weights[2]).astype(jnp.bfloat16)
    gating = jax.nn.sigmoid(project(inputs, weights[3]))
    head_size = query_all.shape[-1] // head_count
    query_heads = query_all.reshape(batch_size, query_count, head_count, head_size)
    key_heads = key_all.reshape(batch_size, query_count, head_count, head_size)
    value_heads = value_all.reshape(batch_size, query_count, head_count, head_size)
    scores = jnp.einsum(
        "bqhd,bkhd->bhqk", query_heads, key_heads, preferred_element_type=jnp.float32
    ) * head_size ** (-0.5)
    if early:
        scores = lax.optimization_barrier(scores)
    if bias_table is not None:
        scores = scores + bias_table.astype(jnp.float32)[None]
    scores = scores + key_bias
    softened = jax.nn.softmax(scores, axis=-1).astype(jnp.bfloat16)
    mixed = jnp.einsum("bhqk,bkhd->bqhd", softened, value_heads, preferred_element_type=jnp.float32)
    mixed = mixed.reshape(batch_size, query_count, head_count * head_size)
    gated = (mixed * gating).astype(jnp.bfloat16)
    return jnp.einsum("bqf,fc->bqc", gated, output_map, preferred_element_type=jnp.float32)


def gather_blocks(block, axis, count):
    half = count // 2
    spread = jnp.broadcast_to(block[None], (half,) + block.shape)
    same_core = lax.all_to_all(spread, "chip", 0, 0, tiled=True)
    other_core = lax.ppermute(same_core, "core", [(0, 1), (1, 0)])
    first = lax.axis_index("core") == 0
    received = jnp.where(
        first,
        jnp.stack([same_core, other_core], axis=1),
        jnp.stack([other_core, same_core], axis=1),
    ).reshape((count,) + block.shape)
    received = jnp.moveaxis(received, 0, axis)
    shape = block.shape[:axis] + (count * block.shape[axis],) + block.shape[axis + 1 :]
    return received.reshape(shape)


def exchange_pair(pair_one, end_local, count):
    rows, width, channels = pair_one.shape
    block = width // count
    pair_part = jnp.moveaxis(pair_one.reshape(rows, count, block, channels), 1, 0)
    pair_part = pair_part.reshape(count, rows * block, channels)
    end_part = jnp.broadcast_to(
        end_local.reshape(1, -1, channels), (count, end_local.size // channels, channels)
    )
    received = lax.all_to_all(
        jnp.concatenate([pair_part, end_part], axis=1), DAP, 0, 0, tiled=True
    )
    pair_cols = received[:, : rows * block].reshape(count * rows, block, channels)
    end_all = received[:, rows * block :].reshape((count,) + end_local.shape)
    end_all = jnp.moveaxis(end_all, 0, 1).reshape(
        (end_local.shape[0], count * end_local.shape[1]) + end_local.shape[2:]
    )
    return pair_cols, end_all


def per_device(
    alignment,
    pairwise,
    sequence_mask,
    residue_mask,
    row_project,
    row_bias_map,
    row_output,
    column_project,
    column_output,
    start_project,
    start_bias_map,
    start_output,
    end_project,
    end_bias_map,
    end_output,
    outer_left,
    outer_right,
    outer_output,
    count=1,
):
    residue_keys = key_offsets(residue_mask)
    sequence_keys = key_offsets(sequence_mask)
    pair_norm = layer_norm(pairwise)
    both_maps = jnp.concatenate([row_bias_map, start_bias_map], axis=1)
    both_local = jnp.einsum(
        "ijc,ch->hij", pair_norm, both_maps, preferred_element_type=jnp.float32
    ).astype(jnp.bfloat16)
    both_bias = gather_blocks(both_local, 1, count)
    row_bias = both_bias[:H_M]
    start_bias = both_bias[H_M:]
    row_update = attend(
        layer_norm(alignment), row_project, row_bias, residue_keys, row_output, H_M, True
    )
    alignment_one = (alignment.astype(jnp.float32) + row_update).astype(jnp.bfloat16)
    alignment_cols = lax.all_to_all(alignment_one, DAP, 1, 0, tiled=True)
    start_update = attend(pair_norm, start_project, start_bias, residue_keys, start_output, H_Z)
    pair_one = (pairwise.astype(jnp.float32) + start_update).astype(jnp.bfloat16)
    rows_norm_one = layer_norm(pair_one)
    end_local = jnp.einsum(
        "kic,ch->hki", rows_norm_one, end_bias_map, preferred_element_type=jnp.float32
    ).astype(jnp.bfloat16)
    pair_cols, end_all = exchange_pair(pair_one, end_local, count)
    end_bias = jnp.swapaxes(end_all, 1, 2)
    column_norm = jnp.swapaxes(layer_norm(alignment_cols), 0, 1)
    column_update = attend(column_norm, column_project, None, sequence_keys, column_output, H_M)
    alignment_out = (alignment_cols.astype(jnp.float32) + jnp.swapaxes(column_update, 0, 1)).astype(
        jnp.bfloat16
    )
    end_norm = jnp.swapaxes(layer_norm(pair_cols), 0, 1)
    end_update = jnp.swapaxes(
        attend(end_norm, end_project, end_bias, residue_keys, end_output, H_Z), 0, 1
    )
    last_norm = layer_norm(alignment_out)
    weighting = sequence_mask.astype(jnp.float32)[:, None, None]
    left = (
        jnp.einsum("sic,co->sio", last_norm, outer_left, preferred_element_type=jnp.float32)
        * weighting
    ).astype(jnp.bfloat16)
    right = (
        jnp.einsum("sic,co->sio", last_norm, outer_right, preferred_element_type=jnp.float32)
        * weighting
    ).astype(jnp.bfloat16)
    row_count = jnp.sum(sequence_mask.astype(jnp.float32))
    outer_sum = (
        jnp.einsum(
            "sic,sje->ijce",
            gather_blocks(left, 1, count),
            right,
            preferred_element_type=jnp.float32,
        )
        / row_count
    )
    flattened = outer_sum.astype(jnp.bfloat16).reshape(outer_sum.shape[0], outer_sum.shape[1], -1)
    outer_update = jnp.einsum(
        "ijf,fc->ijc", flattened, outer_output, preferred_element_type=jnp.float32
    )
    pairwise_out = (pair_cols.astype(jnp.float32) + end_update + outer_update).astype(jnp.bfloat16)
    return (alignment_out, pairwise_out)


def solution(mesh):
    count = mesh.shape["dap"]
    split_mesh = jax.sharding.Mesh(
        mesh.devices.reshape(mesh.shape["grp"], count // 2, 2), ("grp",) + DAP
    )
    return jax.shard_map(
        functools.partial(per_device, count=count),
        mesh=split_mesh,
        in_specs=(
            P(("grp",) + DAP, None, None),
            P(("grp",) + DAP, None, None),
            P("grp"),
            P("grp"),
            P(),
            P(),
            P(),
            P(),
            P(),
            P(),
            P(),
            P(),
            P(),
            P(),
            P(),
            P(),
            P(),
            P(),
        ),
        out_specs=(P("grp", DAP, None), P("grp", DAP, None)),
        check_vma=False,
    )
```

```python
import functools

import jax
import jax.numpy as jnp
from jax import lax
from jax.sharding import PartitionSpec as P

H_M = 8
H_Z = 4
DAP = ("chip", "core")


norm_epsilon = 1e-05
mask_scale = 1000000000.0


def layer_norm(values):
    widened = values.astype(jnp.float32)
    center = widened - jnp.mean(widened, axis=-1, keepdims=True)
    spread = jnp.mean(center * center, axis=-1, keepdims=True)
    return (center * lax.rsqrt(spread + norm_epsilon)).astype(jnp.bfloat16)


def key_offsets(mask_values):
    return (mask_values.astype(jnp.float32) - 1.0) * mask_scale


def project(inputs, weight_table):
    return jnp.einsum("bqc,cf->bqf", inputs, weight_table, preferred_element_type=jnp.float32)


def attend(inputs, weights, bias_table, key_bias, output_map, head_count, blocks=0):
    batch_size, query_count, width = inputs.shape
    query_all = project(inputs, weights[0]).astype(jnp.bfloat16)
    key_all = project(inputs, weights[1]).astype(jnp.bfloat16)
    value_all = project(inputs, weights[2]).astype(jnp.bfloat16)
    gating = jax.nn.sigmoid(project(inputs, weights[3]))
    head_size = query_all.shape[-1] // head_count
    query_heads = query_all.reshape(batch_size, query_count, head_count, head_size)
    key_heads = key_all.reshape(batch_size, query_count, head_count, head_size)
    value_heads = value_all.reshape(batch_size, query_count, head_count, head_size)
    scores = jnp.einsum(
        "bqhd,bkhd->bhqk", query_heads, key_heads, preferred_element_type=jnp.float32
    ) * head_size ** (-0.5)
    if bias_table is not None:
        scores = scores + bias_table.astype(jnp.float32)[None]
    scores = scores + key_bias
    softened = jax.nn.softmax(scores, axis=-1).astype(jnp.bfloat16)
    mixed = jnp.einsum("bhqk,bkhd->bqhd", softened, value_heads, preferred_element_type=jnp.float32)
    mixed = mixed.reshape(batch_size, query_count, head_count * head_size)
    gated = (mixed * gating).astype(jnp.bfloat16)
    if blocks:
        gated = gated.reshape(batch_size, blocks, query_count // blocks, gated.shape[-1])
        return jnp.einsum("bdqf,fc->dbqc", gated, output_map, preferred_element_type=jnp.float32)
    return jnp.einsum("bqf,fc->bqc", gated, output_map, preferred_element_type=jnp.float32)


def gather_blocks(block, axis, count):
    half = count // 2
    spread = jnp.broadcast_to(block[None], (half,) + block.shape)
    same_core = lax.all_to_all(spread, "chip", 0, 0, tiled=True)
    other_core = lax.ppermute(same_core, "core", [(0, 1), (1, 0)])
    first = lax.axis_index("core") == 0
    received = jnp.where(
        first,
        jnp.stack([same_core, other_core], axis=1),
        jnp.stack([other_core, same_core], axis=1),
    ).reshape((count,) + block.shape)
    received = jnp.moveaxis(received, 0, axis)
    shape = block.shape[:axis] + (count * block.shape[axis],) + block.shape[axis + 1 :]
    return received.reshape(shape)


def exchange_pair(pair_one, end_local, count):
    rows, width, channels = pair_one.shape
    block = width // count
    pair_part = jnp.moveaxis(pair_one.reshape(rows, count, block, channels), 1, 0)
    pair_part = pair_part.reshape(count, rows * block, channels)
    end_part = jnp.broadcast_to(
        end_local.reshape(1, -1, channels), (count, end_local.size // channels, channels)
    )
    received = lax.all_to_all(
        jnp.concatenate([pair_part, end_part], axis=1), DAP, 0, 0, tiled=True
    )
    pair_cols = received[:, : rows * block].reshape(count * rows, block, channels)
    end_all = received[:, rows * block :].reshape((count,) + end_local.shape)
    end_all = jnp.moveaxis(end_all, 0, 1).reshape(
        (end_local.shape[0], count * end_local.shape[1]) + end_local.shape[2:]
    )
    return pair_cols, end_all


def per_device(
    alignment,
    pairwise,
    sequence_mask,
    residue_mask,
    row_project,
    row_bias_map,
    row_output,
    column_project,
    column_output,
    start_project,
    start_bias_map,
    start_output,
    end_project,
    end_bias_map,
    end_output,
    outer_left,
    outer_right,
    outer_output,
    count=1,
):
    residue_keys = key_offsets(residue_mask)
    sequence_keys = key_offsets(sequence_mask)
    pair_norm = layer_norm(pairwise)
    both_maps = jnp.concatenate([row_bias_map, start_bias_map], axis=1)
    both_local = jnp.einsum(
        "ijc,ch->hij", pair_norm, both_maps, preferred_element_type=jnp.float32
    ).astype(jnp.bfloat16)
    both_bias = gather_blocks(both_local, 1, count)
    row_bias = both_bias[:H_M]
    start_bias = both_bias[H_M:]
    row_update = attend(
        layer_norm(alignment), row_project, row_bias, residue_keys, row_output, H_M, count
    )
    by_device = jnp.moveaxis(
        alignment.reshape(alignment.shape[0], count, -1, alignment.shape[2]), 1, 0
    )
    alignment_one = (by_device.astype(jnp.float32) + row_update).astype(jnp.bfloat16)
    alignment_cols = lax.all_to_all(alignment_one, DAP, 0, 0, tiled=True)
    alignment_cols = alignment_cols.reshape((-1,) + alignment_cols.shape[2:])
    start_update = attend(pair_norm, start_project, start_bias, residue_keys, start_output, H_Z)
    pair_one = (pairwise.astype(jnp.float32) + start_update).astype(jnp.bfloat16)
    rows_norm_one = layer_norm(pair_one)
    end_local = jnp.einsum(
        "kic,ch->hki", rows_norm_one, end_bias_map, preferred_element_type=jnp.float32
    ).astype(jnp.bfloat16)
    pair_cols, end_all = exchange_pair(pair_one, end_local, count)
    end_bias = jnp.swapaxes(end_all, 1, 2)
    column_norm = jnp.swapaxes(layer_norm(alignment_cols), 0, 1)
    column_update = attend(column_norm, column_project, None, sequence_keys, column_output, H_M)
    alignment_out = (alignment_cols.astype(jnp.float32) + jnp.swapaxes(column_update, 0, 1)).astype(
        jnp.bfloat16
    )
    end_norm = jnp.swapaxes(layer_norm(pair_cols), 0, 1)
    end_update = jnp.swapaxes(
        attend(end_norm, end_project, end_bias, residue_keys, end_output, H_Z), 0, 1
    )
    last_norm = layer_norm(alignment_out)
    weighting = sequence_mask.astype(jnp.float32)[:, None, None]
    left = (
        jnp.einsum("sic,co->sio", last_norm, outer_left, preferred_element_type=jnp.float32)
        * weighting
    ).astype(jnp.bfloat16)
    right = (
        jnp.einsum("sic,co->sio", last_norm, outer_right, preferred_element_type=jnp.float32)
        * weighting
    ).astype(jnp.bfloat16)
    row_count = jnp.sum(sequence_mask.astype(jnp.float32))
    outer_sum = (
        jnp.einsum(
            "sic,sje->ijce",
            gather_blocks(left, 1, count),
            right,
            preferred_element_type=jnp.float32,
        )
        / row_count
    )
    flattened = outer_sum.astype(jnp.bfloat16).reshape(outer_sum.shape[0], outer_sum.shape[1], -1)
    outer_update = jnp.einsum(
        "ijf,fc->ijc", flattened, outer_output, preferred_element_type=jnp.float32
    )
    pairwise_out = (pair_cols.astype(jnp.float32) + end_update + outer_update).astype(jnp.bfloat16)
    return (alignment_out, pairwise_out)


def solution(mesh):
    count = mesh.shape["dap"]
    split_mesh = jax.sharding.Mesh(
        mesh.devices.reshape(mesh.shape["grp"], count // 2, 2), ("grp",) + DAP
    )
    return jax.shard_map(
        functools.partial(per_device, count=count),
        mesh=split_mesh,
        in_specs=(
            P(("grp",) + DAP, None, None),
            P(("grp",) + DAP, None, None),
            P("grp"),
            P("grp"),
            P(),
            P(),
            P(),
            P(),
            P(),
            P(),
            P(),
            P(),
            P(),
            P(),
            P(),
            P(),
            P(),
            P(),
        ),
        out_specs=(P("grp", DAP, None), P("grp", DAP, None)),
        check_vma=False,
    )
```

```python
import functools

import jax
import jax.numpy as jnp
from jax import lax
from jax.sharding import PartitionSpec as P

H_M = 8
H_Z = 4
DAP = ("chip", "core")


norm_epsilon = 1e-05
mask_scale = 1000000000.0


def layer_norm(values):
    widened = values.astype(jnp.float32)
    center = widened - jnp.mean(widened, axis=-1, keepdims=True)
    spread = jnp.mean(center * center, axis=-1, keepdims=True)
    return (center * lax.rsqrt(spread + norm_epsilon)).astype(jnp.bfloat16)


def key_offsets(mask_values):
    return (mask_values.astype(jnp.float32) - 1.0) * mask_scale


def project(inputs, weight_table):
    return jnp.einsum("bqc,cf->bqf", inputs, weight_table, preferred_element_type=jnp.float32)


def attend(inputs, weights, bias_table, key_bias, output_map, head_count):
    batch_size, query_count, width = inputs.shape
    query_all = project(inputs, weights[0]).astype(jnp.bfloat16)
    key_all = project(inputs, weights[1]).astype(jnp.bfloat16)
    value_all = project(inputs, weights[2]).astype(jnp.bfloat16)
    gating = jax.nn.sigmoid(project(inputs, weights[3]))
    head_size = query_all.shape[-1] // head_count
    query_heads = query_all.reshape(batch_size, query_count, head_count, head_size)
    key_heads = key_all.reshape(batch_size, query_count, head_count, head_size)
    value_heads = value_all.reshape(batch_size, query_count, head_count, head_size)
    scores = jnp.einsum(
        "bqhd,bkhd->bhqk", query_heads, key_heads, preferred_element_type=jnp.float32
    ) * head_size ** (-0.5)
    if bias_table is not None:
        scores = scores + bias_table.astype(jnp.float32)[None]
    scores = scores + key_bias
    softened = jax.nn.softmax(scores, axis=-1).astype(jnp.bfloat16)
    mixed = jnp.einsum("bhqk,bkhd->bqhd", softened, value_heads, preferred_element_type=jnp.float32)
    mixed = mixed.reshape(batch_size, query_count, head_count * head_size)
    gated = (mixed * gating).astype(jnp.bfloat16)
    return jnp.einsum("bqf,fc->bqc", gated, output_map, preferred_element_type=jnp.float32)


def gather_blocks(block, axis, count):
    half = count // 2
    spread = jnp.broadcast_to(block[None], (half,) + block.shape)
    same_core = lax.all_to_all(spread, "chip", 0, 0, tiled=True)
    other_core = lax.ppermute(same_core, "core", [(0, 1), (1, 0)])
    first = lax.axis_index("core") == 0
    received = jnp.where(
        first,
        jnp.stack([same_core, other_core], axis=1),
        jnp.stack([other_core, same_core], axis=1),
    ).reshape((count,) + block.shape)
    received = jnp.moveaxis(received, 0, axis)
    shape = block.shape[:axis] + (count * block.shape[axis],) + block.shape[axis + 1 :]
    return received.reshape(shape)


def exchange_pair(pair_one, end_local, count):
    rows, width, channels = pair_one.shape
    block = width // count
    pair_part = jnp.moveaxis(pair_one.reshape(rows, count, block, channels), 1, 0)
    pair_part = pair_part.reshape(count, rows * block, channels)
    end_part = jnp.broadcast_to(
        end_local.reshape(1, -1, channels), (count, end_local.size // channels, channels)
    )
    received = lax.all_to_all(
        jnp.concatenate([pair_part, end_part], axis=1), DAP, 0, 0, tiled=True
    )
    pair_cols = received[:, : rows * block].reshape(count * rows, block, channels)
    end_all = received[:, rows * block :].reshape((count,) + end_local.shape)
    end_all = jnp.moveaxis(end_all, 0, 1).reshape(
        (end_local.shape[0], count * end_local.shape[1]) + end_local.shape[2:]
    )
    return pair_cols, end_all


def per_device(
    alignment,
    pairwise,
    sequence_mask,
    residue_mask,
    row_project,
    row_bias_map,
    row_output,
    column_project,
    column_output,
    start_project,
    start_bias_map,
    start_output,
    end_project,
    end_bias_map,
    end_output,
    outer_left,
    outer_right,
    outer_output,
    count=1,
):
    residue_keys = key_offsets(residue_mask)
    sequence_keys = key_offsets(sequence_mask)
    pair_norm = layer_norm(pairwise)
    both_maps = jnp.concatenate([row_bias_map, start_bias_map], axis=1)
    both_local = jnp.einsum(
        "ijc,ch->hij", pair_norm, both_maps, preferred_element_type=jnp.float32
    ).astype(jnp.bfloat16)
    both_bias = gather_blocks(both_local, 1, count)
    row_bias = both_bias[:H_M]
    start_bias = both_bias[H_M:]
    row_update = attend(layer_norm(alignment), row_project, row_bias, residue_keys, row_output, H_M)
    alignment_one = (alignment.astype(jnp.float32) + row_update).astype(jnp.bfloat16)
    alignment_cols = lax.all_to_all(alignment_one, DAP, 1, 0, tiled=True)
    start_update = attend(pair_norm, start_project, start_bias, residue_keys, start_output, H_Z)
    pair_one = (pairwise.astype(jnp.float32) + start_update).astype(jnp.bfloat16)
    rows_norm_one = layer_norm(pair_one)
    end_local = jnp.einsum(
        "kic,ch->hki", rows_norm_one, end_bias_map, preferred_element_type=jnp.float32
    ).astype(jnp.bfloat16)
    pair_cols = lax.all_to_all(pair_one, DAP, 1, 0, tiled=True)
    column_norm = jnp.swapaxes(layer_norm(alignment_cols), 0, 1)
    column_update = attend(column_norm, column_project, None, sequence_keys, column_output, H_M)
    alignment_out = (alignment_cols.astype(jnp.float32) + jnp.swapaxes(column_update, 0, 1)).astype(
        jnp.bfloat16
    )
    last_norm = layer_norm(alignment_out)
    weighting = sequence_mask.astype(jnp.float32)[:, None, None]
    left = (
        jnp.einsum("sic,co->sio", last_norm, outer_left, preferred_element_type=jnp.float32)
        * weighting
    ).astype(jnp.bfloat16)
    right = (
        jnp.einsum("sic,co->sio", last_norm, outer_right, preferred_element_type=jnp.float32)
        * weighting
    ).astype(jnp.bfloat16)
    row_count = jnp.sum(sequence_mask.astype(jnp.float32))
    packed = jnp.concatenate([left.reshape(-1), end_local.reshape(-1)])
    received = gather_blocks(packed[None], 0, count)
    left_all = jnp.moveaxis(received[:, : left.size].reshape((count,) + left.shape), 0, 1)
    left_all = left_all.reshape(left.shape[0], count * left.shape[1], left.shape[2])
    end_all = jnp.moveaxis(received[:, left.size :].reshape((count,) + end_local.shape), 0, 1)
    end_all = end_all.reshape(
        (end_local.shape[0], count * end_local.shape[1]) + end_local.shape[2:]
    )
    end_bias = jnp.swapaxes(end_all, 1, 2)
    end_norm = jnp.swapaxes(layer_norm(pair_cols), 0, 1)
    end_update = jnp.swapaxes(
        attend(end_norm, end_project, end_bias, residue_keys, end_output, H_Z), 0, 1
    )
    outer_sum = (
        jnp.einsum("sic,sje->ijce", left_all, right, preferred_element_type=jnp.float32)
        / row_count
    )
    flattened = outer_sum.astype(jnp.bfloat16).reshape(outer_sum.shape[0], outer_sum.shape[1], -1)
    outer_update = jnp.einsum(
        "ijf,fc->ijc", flattened, outer_output, preferred_element_type=jnp.float32
    )
    pairwise_out = (pair_cols.astype(jnp.float32) + end_update + outer_update).astype(jnp.bfloat16)
    return (alignment_out, pairwise_out)


def solution(mesh):
    count = mesh.shape["dap"]
    split_mesh = jax.sharding.Mesh(
        mesh.devices.reshape(mesh.shape["grp"], count // 2, 2), ("grp",) + DAP
    )
    return jax.shard_map(
        functools.partial(per_device, count=count),
        mesh=split_mesh,
        in_specs=(
            P(("grp",) + DAP, None, None),
            P(("grp",) + DAP, None, None),
            P("grp"),
            P("grp"),
            P(),
            P(),
            P(),
            P(),
            P(),
            P(),
            P(),
            P(),
            P(),
            P(),
            P(),
            P(),
            P(),
            P(),
        ),
        out_specs=(P("grp", DAP, None), P("grp", DAP, None)),
        check_vma=False,
    )
```
